256 devices in a mesh: expert: 32 (over x, z), tensor: 8 (over y, core).
Axes of the slice: x: 4, y: 4, z: 8, core: 2. Of those that a mesh axis runs over, the one named last changes fastest.
Arguments:
- attn_vals: bfloat16 [2048, 4096], P('expert', 'tensor'), may hold values from -6 to 6
- residual: bfloat16 [2048, 4096], P('expert', 'tensor'), may hold values from -6 to 6
- out_weight: bfloat16 [4096, 4096], P('tensor'), may hold values from -0.09375 to 0.09375
- norm_gain: float32 [4096], P('tensor'), may hold values from 0.5 to 1.5
- router_weight: float32 [4096, 8], P('tensor'), may hold values from -0.09375 to 0.09375
- routes: int32 [2048, 2], P('expert'), may hold values from 0 to 7, all different within a row; in each aligned block of 64 rows (0 to 63, 64 to 127, ...) at most 32 rows name the same one
- w_gate: bfloat16 [32, 4096, 2048], P('expert', None, 'tensor'), may hold values from -0.09375 to 0.09375
- w_up: bfloat16 [32, 4096, 2048], P('expert', None, 'tensor'), may hold values from -0.09375 to 0.09375
- w_down: bfloat16 [32, 2048, 4096], P('expert', 'tensor'), may hold values from -0.0625 to 0.0625
- slab_of: int32 [32], replicated, may hold values from 0 to 31, each once
- final_gain: float32 [4096], P('tensor'), may hold values from 0.5 to 1.5
- row_order: int32 [2048], replicated, may hold values from 0 to 2047, each once
Outputs:
- stream_out: bfloat16 [2048, 4096], P('expert', 'tensor')
- normed_out: bfloat16 [2048, 4096], P('expert', 'tensor')
The draws below stay inside these ranges and needn't reach their ends.
Inputs may be any that keep to these rules, and one draw needn't show every extreme that they name: `routes`: the two experts of a row differ. In each aligned block of 64 rows (the rows of one device) no expert is named by more than 32 rows, and some block names one expert exactly 32 times. `slab_of`: A permutation. `row_order`: A permutation.
All inputs are finite; a program needn't handle non-finite values.
Results may differ from the reference program's by a relative error of at most 0.017.
Values may be sent and summed in bfloat16 or wider, within the bound.
No kernel may reach another device: no remote copies, remote signals or barrier semaphores. Data moves between devices by JAX's collectives and lax.ppermute only.
A program may use at most 128 MiB of HBM per device.

```python
import math
import jax
import jax.numpy as jnp
import numpy as np
from jax import lax

D = 4096
FF = 8192
EXPERTS = 8
ROWS_DEV = 64
MOST = 32
ROWS = 2048
FFS = 2048
N_EXPERT = 32
N_TENSOR = 8


def steps_of(rng, extent, cuts, least, high):
    def one(position, shards_of):
        heights = jax.random.uniform(jax.random.fold_in(jax.random.fold_in(rng, 6), position), (shards_of,), jnp.float32, least / len(cuts), high / len(cuts))
        return jnp.repeat(jnp.exp(heights), extent[position] // shards_of).reshape((-1,) + (1,) * (len(extent) - position - 1))

    gain = one(*cuts[0])
    for cut in cuts[1:]:
        gain = gain * one(*cut)
    return gain


def routed_block(rng, own, number, rows, count, top, bound, skew):
    sequence = jax.random.permutation(rng, count)
    crowded, usual = shares(count, rows * top, bound, skew, True), shares(count, rows * top, bound, skew, False)
    places = jnp.arange(count)

    def named(tallies, turn):
        used = int((tallies > 0).sum())
        fixed = max(1, used // 4)
        passed = fixed + (places - fixed + turn * (used - fixed)) % max(1, count - fixed)
        return jnp.zeros((count,), jnp.int32).at[sequence[jnp.where(places < fixed, places, passed)]].set(jnp.asarray(tallies, jnp.int32))

    tallies = jnp.where(number % 4 == 0, named(crowded, number // 4), named(usual, number - number // 4 - 1))
    mixed = jax.random.permutation(jax.random.fold_in(own, 3), count)
    giver, receiver = mixed[0:count // 2 * 2:2], mixed[1:count // 2 * 2:2]
    margin = jnp.minimum(tallies[giver] - 1, bound - tallies[receiver]) // 2
    margin = jnp.where((giver == sequence[0]) | (receiver == sequence[0]) | (tallies[receiver] == 0), 0, jnp.maximum(margin, 0))
    passed = jax.random.randint(jax.random.fold_in(own, 4), (count // 2,), 0, 1 << 20) % (margin + 1)
    tallies = tallies.at[giver].add(-passed).at[receiver].add(passed)
    items = jnp.searchsorted(jnp.cumsum(tallies), jnp.arange(rows * top), side="right").astype(jnp.int32)
    grid = items.reshape(top, rows).T
    grid = grid[jax.random.permutation(jax.random.fold_in(own, 1), rows)]
    turn = jax.random.randint(jax.random.fold_in(own, 2), (rows, 1), 0, top)
    return jnp.take_along_axis(grid, (jnp.arange(top)[None, :] + turn) % top, axis=1)


def shares(count, total, most, slope, full):
    loads = [(1 << 20) // math.isqrt(grade ** slope) + 1 for grade in range(1, count + 1)]
    largest = most if full else min(most, max(-(-total // count), total * loads[0] // sum(loads)))
    least = 1 if total - largest >= count - 1 else 0
    counts, spare = [largest] + [least] * (count - 1), total - largest - least * (count - 1)
    while spare > 0:
        free = [i for i in range(1, count) if counts[i] < largest] or [i for i in range(1, count) if counts[i] < most]
        pool, left = sum([loads[i] for i in free]), spare
        for i in free:
            addition = min(most - counts[i], max(1, left * loads[i] // pool), spare)
            counts[i] = counts[i] + addition
            spare = spare - addition
    return np.array(counts)


def scatter_about(stream_key, shape, deviation, most, cuts=(), kind=jnp.bfloat16):
    entries = jax.random.normal(stream_key, shape, jnp.float32) * deviation
    if len(cuts) > 0:
        entries = steps_of(stream_key, shape, cuts, -0.22, 0.18) * entries
    return jnp.clip(entries, min=-most, max=most).astype(kind)


def setup_inputs(seed: int = 0) -> dict:
    splits = jax.random.split(jax.random.key(seed), 13)
    attn_vals = scatter_about(splits[0], (ROWS, D), 1.0, 6.0, ((0, 32), (1, 8)))
    residual = scatter_about(splits[1], (ROWS, D), 1.0, 6.0, ((0, 32), (1, 8)))
    out_weight = scatter_about(splits[2], (D, D), D ** -0.5, 0.09375, ((0, 8),))
    norm_gain = jnp.clip(1.0 + 0.1 * jax.random.normal(splits[3], (D,), jnp.float32), 0.5, 1.5)
    router_weight = scatter_about(splits[4], (D, EXPERTS), D ** -0.5, 0.09375, ((0, 8),), jnp.float32)
    routes_keys = jax.random.split(jax.random.fold_in(splits[5], 1), ROWS // ROWS_DEV)
    routes_turns = jax.random.permutation(jax.random.fold_in(splits[5], 3), ROWS // ROWS_DEV)
    routes = jax.vmap(lambda own, number: routed_block(jax.random.fold_in(splits[5], 2), own, number, ROWS_DEV, EXPERTS, 2, MOST, 2))(routes_keys, routes_turns).reshape((ROWS, 2))
    w_gate = scatter_about(splits[6], (N_EXPERT, D, FFS), D ** -0.5, 0.09375, ((0, 32), (2, 8)))
    w_up = scatter_about(splits[7], (N_EXPERT, D, FFS), D ** -0.5, 0.09375, ((0, 32), (2, 8)))
    w_down = scatter_about(splits[8], (N_EXPERT, FFS, D), FF ** -0.5, 0.0625, ((0, 32), (1, 8)))
    slab_of = jax.random.permutation(splits[9], N_EXPERT).astype(jnp.int32)
    final_gain = jnp.clip(1.0 + 0.1 * jax.random.normal(splits[10], (D,), jnp.float32), 0.5, 1.5)
    row_order = jax.random.permutation(splits[11], ROWS).astype(jnp.int32)
    return {"attn_vals": attn_vals, "residual": residual, "out_weight": out_weight, "norm_gain": norm_gain, "router_weight": router_weight, "routes": routes, "w_gate": w_gate, "w_up": w_up, "w_down": w_down, "slab_of": slab_of, "final_gain": final_gain, "row_order": row_order}


EPS = 1e-05

def reference(attn_vals, residual, out_weight, norm_gain, router_weight, routes, w_gate, w_up, w_down, slab_of, final_gain, row_order):
    project = jnp.dot(attn_vals, out_weight, preferred_element_type=jnp.float32)
    stream_in = (residual.astype(jnp.float32) + project).astype(jnp.bfloat16)
    hidden_f = stream_in.astype(jnp.float32)
    scaled = hidden_f * norm_gain
    inverse_rms = lax.rsqrt(lax.optimization_barrier(jnp.mean(hidden_f * hidden_f, axis=1)) + EPS)
    normed_in = (scaled * inverse_rms[:, None]).astype(jnp.bfloat16)
    logits = jnp.dot(scaled, router_weight, precision=lax.Precision.HIGHEST) * inverse_rms[:, None]
    chosen = jnp.take_along_axis(logits, routes, axis=1)
    leading = jax.nn.sigmoid(chosen[:, 0] - chosen[:, 1])
    mixing = jnp.stack([leading, 1.0 - leading], axis=1)
    slab_count = N_EXPERT // EXPERTS
    per_block = FF // (slab_count * N_TENSOR)
    holders = jnp.zeros((N_EXPERT,), jnp.int32).at[slab_of].set(jnp.arange(N_EXPERT, dtype=jnp.int32))
    holders = holders.reshape(EXPERTS, slab_count)
    capacity = N_EXPERT * MOST

    def one_expert(totals, expert):
        picked = routes == expert
        member = jnp.any(picked, axis=1)
        index_list = jnp.nonzero(member, size=capacity, fill_value=0)[0].astype(jnp.int32)
        valid = (jnp.arange(capacity) < jnp.sum(member.astype(jnp.int32))).astype(jnp.float32)
        inputs = normed_in[index_list].astype(jnp.float32)
        owner = holders[expert]
        gate_val = jnp.einsum('cd,sdf->csf', inputs, w_gate[owner].astype(jnp.float32))
        up_val = jnp.einsum('cd,sdf->csf', inputs, w_up[owner].astype(jnp.float32))
        active = (jax.nn.silu(gate_val) * up_val).astype(jnp.bfloat16)
        active = active.reshape(capacity, slab_count, N_TENSOR, per_block).astype(jnp.float32)
        down_w = w_down[owner].reshape(slab_count, N_TENSOR, per_block, D).astype(jnp.float32)
        pieces = jnp.einsum('cstf,stfd->cstd', active, down_w).astype(jnp.bfloat16)
        pieces = lax.optimization_barrier(pieces)
        slab_sum = lax.optimization_barrier(jnp.sum(pieces.astype(jnp.float32), axis=2)).astype(jnp.bfloat16)
        slab_sum = lax.optimization_barrier(slab_sum)
        output = lax.optimization_barrier(jnp.sum(slab_sum.astype(jnp.float32), axis=1))
        factor = lax.optimization_barrier(jnp.sum(jnp.where(picked[index_list], mixing[index_list], 0.0), axis=1)) * valid
        return (totals.at[index_list].add(output * factor[:, None]), None)
    blended, _ = lax.scan(one_expert, jnp.zeros((ROWS, D), jnp.float32), jnp.arange(EXPERTS, dtype=jnp.int32))
    stream = (hidden_f + blended).astype(jnp.bfloat16)
    stream_f = stream.astype(jnp.float32)
    final_rms = lax.rsqrt(lax.optimization_barrier(jnp.mean(stream_f * stream_f, axis=1)) + EPS)
    normed = (stream_f * final_rms[:, None] * final_gain).astype(jnp.bfloat16)
    source = jnp.zeros((ROWS,), jnp.int32).at[row_order].set(jnp.arange(ROWS, dtype=jnp.int32))
    return (stream[source], normed[source])
```

```python
import jax
import jax.numpy as jnp
from jax import lax
from jax.sharding import PartitionSpec as P

D = 4096
MOST = 32


EPS = 1e-05


def finish_slots(gate_val, up_val, down_weight):
    active = (jax.nn.silu(gate_val) * up_val).astype(jnp.bfloat16)
    partial_out = jnp.einsum("gmf,fd->gmd", active, down_weight, preferred_element_type=jnp.float32)
    summed = lax.psum_scatter(
        partial_out.astype(jnp.bfloat16), "tensor", scatter_dimension=2, tiled=True
    )
    return lax.all_to_all(summed, "expert", split_axis=0, concat_axis=0, tiled=True)


def final_norm(stream, final_gain):
    stream_f = stream.astype(jnp.float32)
    square_total = lax.psum(jnp.sum(stream_f * stream_f, axis=1), "tensor")
    factor = lax.rsqrt(square_total / D + EPS)
    return (stream_f * factor[:, None] * final_gain).astype(jnp.bfloat16)


def on_device(
    attn_vals,
    residual,
    out_weight,
    norm_gain,
    router_weight,
    routes,
    w_gate,
    w_up,
    w_down,
    slab_of,
    final_gain,
    row_order,
):
    groups = lax.axis_size("expert")
    row_count = attn_vals.shape[0]
    expert_count = router_weight.shape[1]
    slab_count = groups // expert_count
    partial_proj = jnp.dot(attn_vals, out_weight, preferred_element_type=jnp.float32)
    project = lax.psum_scatter(
        partial_proj.astype(jnp.bfloat16), "tensor", scatter_dimension=1, tiled=True
    ).astype(jnp.float32)
    stream_in = (residual.astype(jnp.float32) + project).astype(jnp.bfloat16)
    hidden_f = stream_in.astype(jnp.float32)
    scaled = hidden_f * norm_gain
    square_sum, logit_part = lax.psum(
        (
            jnp.sum(hidden_f * hidden_f, axis=1),
            jnp.dot(scaled, router_weight, precision=lax.Precision.HIGHEST),
        ),
        "tensor",
    )
    inverse_rms = lax.rsqrt(square_sum / D + EPS)
    normed_in = (scaled * inverse_rms[:, None]).astype(jnp.bfloat16)
    logits = logit_part * inverse_rms[:, None]
    expert_ids = jnp.arange(expert_count, dtype=jnp.int32)
    route_hot = (routes[:, :, None] == expert_ids[None, None, :]).astype(jnp.int32)
    chosen = jnp.sum(route_hot.astype(jnp.float32) * logits[:, None, :], axis=2)
    leading = jax.nn.sigmoid(chosen[:, 0] - chosen[:, 1])
    mixing = jnp.stack([leading, 1.0 - leading], axis=1)
    route_hits = jnp.sum(route_hot, axis=1)
    before_count = jnp.cumsum(route_hits, axis=0) - route_hits
    slot_ids = jnp.sum(route_hot * before_count[:, None, :], axis=2)
    slot_hot = (slot_ids[:, :, None] == jnp.arange(MOST, dtype=jnp.int32)[None, None, :]).astype(
        jnp.float32
    )
    placing = jnp.einsum("rke,rks->esr", route_hot.astype(jnp.float32), slot_hot).astype(
        jnp.bfloat16
    )
    target_expert = slab_of // slab_count
    send_map = jnp.take(placing, target_expert, axis=0)
    outgoing = jnp.einsum(
        "gsr,rd->gsd", send_map, normed_in, preferred_element_type=jnp.float32
    ).astype(jnp.bfloat16)
    arrived_part = lax.all_to_all(outgoing, "expert", split_axis=0, concat_axis=0, tiled=True)
    arrived = lax.all_gather(arrived_part, "tensor", axis=2, tiled=True)
    gate_val = jnp.einsum("gmd,df->gmf", arrived, w_gate[0], preferred_element_type=jnp.float32)
    up_val = jnp.einsum("gmd,df->gmf", arrived, w_up[0], preferred_element_type=jnp.float32)
    returned = finish_slots(gate_val, up_val, w_down[0])
    group_ids = jnp.arange(groups, dtype=jnp.int32)
    holder_hot = (slab_of[None, :] == group_ids[:, None]).astype(jnp.int32)
    holders = jnp.sum(holder_hot * group_ids[None, :], axis=1).reshape(expert_count, slab_count)
    row_holders = jnp.take(holders, routes, axis=0)
    flat_index = row_holders * MOST + slot_ids[:, :, None]
    flat_back = returned.reshape(groups * MOST, returned.shape[2])
    fetched = jnp.take(flat_back, flat_index.reshape(-1), axis=0).reshape(
        row_count, 2, slab_count, returned.shape[2]
    )
    expert_out = jnp.sum(fetched.astype(jnp.float32), axis=2)
    blended = jnp.sum(mixing[:, :, None] * expert_out, axis=1)
    stream = (hidden_f + blended).astype(jnp.bfloat16)
    positions = lax.axis_index("expert") * row_count + jnp.arange(row_count, dtype=jnp.int32)
    matches = (row_order[None, :] == positions[:, None]).astype(jnp.int32)
    source = jnp.sum(matches * jnp.arange(row_order.shape[0], dtype=jnp.int32)[None, :], axis=1)
    all_stream = lax.all_gather(stream, "expert", axis=0, tiled=True)
    ordered = jnp.take(all_stream, source, axis=0)
    return (ordered, final_norm(ordered, final_gain))


def solution(mesh):
    return jax.shard_map(
        on_device,
        mesh=mesh,
        in_specs=(
            P("expert", "tensor"),
            P("expert", "tensor"),
            P("tensor", None),
            P("tensor"),
            P("tensor", None),
            P("expert", None),
            P("expert", None, "tensor"),
            P("expert", None, "tensor"),
            P("expert", "tensor", None),
            P(),
            P("tensor"),
            P(),
        ),
        out_specs=(P("expert", "tensor"), P("expert", "tensor")),
        check_vma=False,
    )
```

```python
import jax
import jax.numpy as jnp
from jax import lax
from jax.sharding import Mesh, PartitionSpec as P

D = 4096
MOST = 32


EPS = 1e-05


def finish_slots(gate_val, up_val, down_weight):
    active = (jax.nn.silu(gate_val) * up_val).astype(jnp.bfloat16)
    partial_out = jnp.einsum("gmf,fd->gmd", active, down_weight, preferred_element_type=jnp.float32)
    summed = lax.psum_scatter(
        partial_out.astype(jnp.bfloat16), "tensor", scatter_dimension=2, tiled=True
    )
    return lax.all_to_all(summed, EXPERT, split_axis=0, concat_axis=0, tiled=True)


def final_norm(stream, final_gain):
    stream_f = stream.astype(jnp.float32)
    square_total = lax.psum(jnp.sum(stream_f * stream_f, axis=1), "tensor")
    factor = lax.rsqrt(square_total / D + EPS)
    return (stream_f * factor[:, None] * final_gain).astype(jnp.bfloat16)


EXPERT = ("ex", "ez")


def restore(stream, row_order, source):
    outer = lax.axis_size("ex")
    inner = lax.axis_size("ez")
    rows = stream.shape[0]
    x_idx = lax.axis_index("ex")
    z_idx = lax.axis_index("ez")
    e_idx = x_idx * inner + z_idx
    gathered = lax.all_gather(stream, "ex", axis=0, tiled=True)
    dest = row_order // rows
    held = (
        (jnp.arange(outer, dtype=jnp.int32)[:, None] * inner + z_idx) * rows
        + jnp.arange(rows, dtype=jnp.int32)[None, :]
    ).reshape(-1)
    held_dest = jnp.take(dest, held, axis=0)
    count = held.shape[0]
    order = jnp.arange(count, dtype=jnp.int32)
    earlier = (held_dest[:, None] == held_dest[None, :]) & (order[None, :] < order[:, None])
    held_slot = jnp.sum(earlier.astype(jnp.int32), axis=1)
    mine = (held_dest // inner) == x_idx
    pick = (
        mine[None, None, :]
        & ((held_dest % inner)[None, None, :] == jnp.arange(inner, dtype=jnp.int32)[:, None, None])
        & (held_slot[None, None, :] == jnp.arange(rows, dtype=jnp.int32)[None, :, None])
    ).astype(jnp.bfloat16)
    send = jnp.einsum("zkg,gf->zkf", pick, gathered, preferred_element_type=jnp.float32).astype(
        jnp.bfloat16
    )
    received = lax.all_to_all(send, "ez", split_axis=0, concat_axis=0, tiled=True)
    arrival = jnp.arange(row_order.shape[0], dtype=jnp.int32)
    column = (arrival // rows) % inner
    source_column = (source // rows) % inner
    before = (
        (dest == e_idx)[None, :]
        & (column[None, :] == source_column[:, None])
        & (arrival[None, :] < source[:, None])
    )
    slot = jnp.sum(before.astype(jnp.int32), axis=1)
    flat = received.reshape(inner * rows, received.shape[2])
    return jnp.take(flat, source_column * rows + slot, axis=0)


def on_device(
    attn_vals,
    residual,
    out_weight,
    norm_gain,
    router_weight,
    routes,
    w_gate,
    w_up,
    w_down,
    slab_of,
    final_gain,
    row_order,
):
    groups = lax.axis_size("ex") * lax.axis_size("ez")
    row_count = attn_vals.shape[0]
    expert_count = router_weight.shape[1]
    slab_count = groups // expert_count
    partial_proj = jnp.dot(attn_vals, out_weight, preferred_element_type=jnp.float32)
    project = lax.psum_scatter(
        partial_proj.astype(jnp.bfloat16), "tensor", scatter_dimension=1, tiled=True
    ).astype(jnp.float32)
    stream_in = (residual.astype(jnp.float32) + project).astype(jnp.bfloat16)
    hidden_f = stream_in.astype(jnp.float32)
    scaled = hidden_f * norm_gain
    square_sum, logit_part = lax.psum(
        (
            jnp.sum(hidden_f * hidden_f, axis=1),
            jnp.dot(scaled, router_weight, precision=lax.Precision.HIGHEST),
        ),
        "tensor",
    )
    inverse_rms = lax.rsqrt(square_sum / D + EPS)
    normed_in = (scaled * inverse_rms[:, None]).astype(jnp.bfloat16)
    logits = logit_part * inverse_rms[:, None]
    expert_ids = jnp.arange(expert_count, dtype=jnp.int32)
    route_hot = (routes[:, :, None] == expert_ids[None, None, :]).astype(jnp.int32)
    chosen = jnp.sum(route_hot.astype(jnp.float32) * logits[:, None, :], axis=2)
    leading = jax.nn.sigmoid(chosen[:, 0] - chosen[:, 1])
    mixing = jnp.stack([leading, 1.0 - leading], axis=1)
    route_hits = jnp.sum(route_hot, axis=1)
    before_count = jnp.cumsum(route_hits, axis=0) - route_hits
    slot_ids = jnp.sum(route_hot * before_count[:, None, :], axis=2)
    slot_hot = (slot_ids[:, :, None] == jnp.arange(MOST, dtype=jnp.int32)[None, None, :]).astype(
        jnp.float32
    )
    placing = jnp.einsum("rke,rks->esr", route_hot.astype(jnp.float32), slot_hot).astype(
        jnp.bfloat16
    )
    target_expert = slab_of // slab_count
    send_map = jnp.take(placing, target_expert, axis=0)
    outgoing = jnp.einsum(
        "gsr,rd->gsd", send_map, normed_in, preferred_element_type=jnp.float32
    ).astype(jnp.bfloat16)
    arrived_part = lax.all_to_all(outgoing, EXPERT, split_axis=0, concat_axis=0, tiled=True)
    arrived = lax.all_gather(arrived_part, "tensor", axis=2, tiled=True)
    gate_val = jnp.einsum("gmd,df->gmf", arrived, w_gate[0], preferred_element_type=jnp.float32)
    up_val = jnp.einsum("gmd,df->gmf", arrived, w_up[0], preferred_element_type=jnp.float32)
    returned = finish_slots(gate_val, up_val, w_down[0])
    group_ids = jnp.arange(groups, dtype=jnp.int32)
    holder_hot = (slab_of[None, :] == group_ids[:, None]).astype(jnp.int32)
    holders = jnp.sum(holder_hot * group_ids[None, :], axis=1).reshape(expert_count, slab_count)
    row_holders = jnp.take(holders, routes, axis=0)
    flat_index = row_holders * MOST + slot_ids[:, :, None]
    flat_back = returned.reshape(groups * MOST, returned.shape[2])
    fetched = jnp.take(flat_back, flat_index.reshape(-1), axis=0).reshape(
        row_count, 2, slab_count, returned.shape[2]
    )
    expert_out = jnp.sum(fetched.astype(jnp.float32), axis=2)
    blended = jnp.sum(mixing[:, :, None] * expert_out, axis=1)
    stream = (hidden_f + blended).astype(jnp.bfloat16)
    positions = (lax.axis_index("ex") * lax.axis_size("ez") + lax.axis_index("ez")) * row_count + jnp.arange(row_count, dtype=jnp.int32)
    matches = (row_order[None, :] == positions[:, None]).astype(jnp.int32)
    source = jnp.sum(matches * jnp.arange(row_order.shape[0], dtype=jnp.int32)[None, :], axis=1)
    ordered = restore(stream, row_order, source)
    return (ordered, final_norm(ordered, final_gain))


def outer_size(mesh):
    column = mesh.devices[:, 0]
    try:
        outer = len({d.coords[0] for d in column})
    except AttributeError:
        outer = 1
    if outer < 1 or column.shape[0] % outer:
        outer = 1
    return outer


def solution(mesh):
    outer = outer_size(mesh)
    shape = mesh.devices.shape
    split = Mesh(mesh.devices.reshape(outer, shape[0] // outer, shape[1]), ("ex", "ez", "tensor"))
    return jax.shard_map(
        on_device,
        mesh=split,
        in_specs=(
            P(EXPERT, "tensor"),
            P(EXPERT, "tensor"),
            P("tensor", None),
            P("tensor"),
            P("tensor", None),
            P(EXPERT, None),
            P(EXPERT, None, "tensor"),
            P(EXPERT, None, "tensor"),
            P(EXPERT, "tensor", None),
            P(),
            P("tensor"),
            P(),
        ),
        out_specs=(P(EXPERT, "tensor"), P(EXPERT, "tensor")),
        check_vma=False,
    )
```

```python
import jax
import jax.numpy as jnp
from jax import lax
from jax.sharding import Mesh, PartitionSpec as P

D = 4096
MOST = 32
CHUNKS = 2


EPS = 1e-05


def finish_slots(gate_val, up_val, down_weight):
    active = (jax.nn.silu(gate_val) * up_val).astype(jnp.bfloat16)
    partial_out = jnp.einsum("gmf,fd->gmd", active, down_weight, preferred_element_type=jnp.float32)
    summed = lax.psum_scatter(
        partial_out.astype(jnp.bfloat16), "tensor", scatter_dimension=2, tiled=True
    )
    return lax.all_to_all(summed, EXPERT, split_axis=0, concat_axis=0, tiled=True)


def final_norm(stream, final_gain):
    stream_f = stream.astype(jnp.float32)
    square_total = lax.psum(jnp.sum(stream_f * stream_f, axis=1), "tensor")
    factor = lax.rsqrt(square_total / D + EPS)
    return (stream_f * factor[:, None] * final_gain).astype(jnp.bfloat16)


EXPERT = ("ex", "ez")


def restore(stream, row_order, source):
    outer = lax.axis_size("ex")
    inner = lax.axis_size("ez")
    rows = stream.shape[0]
    x_idx = lax.axis_index("ex")
    z_idx = lax.axis_index("ez")
    e_idx = x_idx * inner + z_idx
    gathered = lax.all_gather(stream, "ex", axis=0, tiled=True)
    dest = row_order // rows
    held = (
        (jnp.arange(outer, dtype=jnp.int32)[:, None] * inner + z_idx) * rows
        + jnp.arange(rows, dtype=jnp.int32)[None, :]
    ).reshape(-1)
    held_dest = jnp.take(dest, held, axis=0)
    count = held.shape[0]
    order = jnp.arange(count, dtype=jnp.int32)
    earlier = (held_dest[:, None] == held_dest[None, :]) & (order[None, :] < order[:, None])
    held_slot = jnp.sum(earlier.astype(jnp.int32), axis=1)
    mine = (held_dest // inner) == x_idx
    pick = (
        mine[None, None, :]
        & ((held_dest % inner)[None, None, :] == jnp.arange(inner, dtype=jnp.int32)[:, None, None])
        & (held_slot[None, None, :] == jnp.arange(rows, dtype=jnp.int32)[None, :, None])
    ).astype(jnp.bfloat16)
    send = jnp.einsum("zkg,gf->zkf", pick, gathered, preferred_element_type=jnp.float32).astype(
        jnp.bfloat16
    )
    received = lax.all_to_all(send, "ez", split_axis=0, concat_axis=0, tiled=True)
    arrival = jnp.arange(row_order.shape[0], dtype=jnp.int32)
    column = (arrival // rows) % inner
    source_column = (source // rows) % inner
    before = (
        (dest == e_idx)[None, :]
        & (column[None, :] == source_column[:, None])
        & (arrival[None, :] < source[:, None])
    )
    slot = jnp.sum(before.astype(jnp.int32), axis=1)
    flat = received.reshape(inner * rows, received.shape[2])
    return jnp.take(flat, source_column * rows + slot, axis=0)


def on_device(
    attn_vals,
    residual,
    out_weight,
    norm_gain,
    router_weight,
    routes,
    w_gate,
    w_up,
    w_down,
    slab_of,
    final_gain,
    row_order,
):
    groups = lax.axis_size("ex") * lax.axis_size("ez")
    row_count = attn_vals.shape[0]
    expert_count = router_weight.shape[1]
    slab_count = groups // expert_count
    partial_proj = jnp.dot(attn_vals, out_weight, preferred_element_type=jnp.float32)
    project = lax.psum_scatter(
        partial_proj.astype(jnp.bfloat16), "tensor", scatter_dimension=1, tiled=True
    ).astype(jnp.float32)
    stream_in = (residual.astype(jnp.float32) + project).astype(jnp.bfloat16)
    hidden_f = stream_in.astype(jnp.float32)
    scaled = hidden_f * norm_gain
    square_sum, logit_part = lax.psum(
        (
            jnp.sum(hidden_f * hidden_f, axis=1),
            jnp.dot(scaled, router_weight, precision=lax.Precision.HIGHEST),
        ),
        "tensor",
    )
    inverse_rms = lax.rsqrt(square_sum / D + EPS)
    normed_in = (scaled * inverse_rms[:, None]).astype(jnp.bfloat16)
    logits = logit_part * inverse_rms[:, None]
    expert_ids = jnp.arange(expert_count, dtype=jnp.int32)
    route_hot = (routes[:, :, None] == expert_ids[None, None, :]).astype(jnp.int32)
    chosen = jnp.sum(route_hot.astype(jnp.float32) * logits[:, None, :], axis=2)
    leading = jax.nn.sigmoid(chosen[:, 0] - chosen[:, 1])
    mixing = jnp.stack([leading, 1.0 - leading], axis=1)
    route_hits = jnp.sum(route_hot, axis=1)
    before_count = jnp.cumsum(route_hits, axis=0) - route_hits
    slot_ids = jnp.sum(route_hot * before_count[:, None, :], axis=2)
    slot_hot = (slot_ids[:, :, None] == jnp.arange(MOST, dtype=jnp.int32)[None, None, :]).astype(
        jnp.float32
    )
    placing = jnp.einsum("rke,rks->esr", route_hot.astype(jnp.float32), slot_hot).astype(
        jnp.bfloat16
    )
    target_expert = slab_of // slab_count
    send_map = jnp.take(placing, target_expert, axis=0)
    outgoing = jnp.einsum(
        "gsr,rd->gsd", send_map, normed_in, preferred_element_type=jnp.float32
    ).astype(jnp.bfloat16)
    step = MOST // CHUNKS
    pieces = []
    for c in range(CHUNKS):
        part = outgoing[:, c * step : (c + 1) * step]
        arrived_part = lax.all_to_all(part, EXPERT, split_axis=0, concat_axis=0, tiled=True)
        arrived = lax.all_gather(arrived_part, "tensor", axis=2, tiled=True)
        gate_val = jnp.einsum("gmd,df->gmf", arrived, w_gate[0], preferred_element_type=jnp.float32)
        up_val = jnp.einsum("gmd,df->gmf", arrived, w_up[0], preferred_element_type=jnp.float32)
        pieces.append(finish_slots(gate_val, up_val, w_down[0]))
    returned = jnp.concatenate(pieces, axis=1)
    group_ids = jnp.arange(groups, dtype=jnp.int32)
    holder_hot = (slab_of[None, :] == group_ids[:, None]).astype(jnp.int32)
    holders = jnp.sum(holder_hot * group_ids[None, :], axis=1).reshape(expert_count, slab_count)
    row_holders = jnp.take(holders, routes, axis=0)
    flat_index = row_holders * MOST + slot_ids[:, :, None]
    flat_back = returned.reshape(groups * MOST, returned.shape[2])
    fetched = jnp.take(flat_back, flat_index.reshape(-1), axis=0).reshape(
        row_count, 2, slab_count, returned.shape[2]
    )
    expert_out = jnp.sum(fetched.astype(jnp.float32), axis=2)
    blended = jnp.sum(mixing[:, :, None] * expert_out, axis=1)
    stream = (hidden_f + blended).astype(jnp.bfloat16)
    positions = (lax.axis_index("ex") * lax.axis_size("ez") + lax.axis_index("ez")) * row_count + jnp.arange(row_count, dtype=jnp.int32)
    matches = (row_order[None, :] == positions[:, None]).astype(jnp.int32)
    source = jnp.sum(matches * jnp.arange(row_order.shape[0], dtype=jnp.int32)[None, :], axis=1)
    ordered = restore(stream, row_order, source)
    return (ordered, final_norm(ordered, final_gain))


def outer_size(mesh):
    column = mesh.devices[:, 0]
    try:
        outer = len({d.coords[0] for d in column})
    except AttributeError:
        outer = 1
    if outer < 1 or column.shape[0] % outer:
        outer = 1
    return outer


def solution(mesh):
    outer = outer_size(mesh)
    shape = mesh.devices.shape
    split = Mesh(mesh.devices.reshape(outer, shape[0] // outer, shape[1]), ("ex", "ez", "tensor"))
    return jax.shard_map(
        on_device,
        mesh=split,
        in_specs=(
            P(EXPERT, "tensor"),
            P(EXPERT, "tensor"),
            P("tensor", None),
            P("tensor"),
            P("tensor", None),
            P(EXPERT, None),
            P(EXPERT, None, "tensor"),
            P(EXPERT, None, "tensor"),
            P(EXPERT, "tensor", None),
            P(),
            P("tensor"),
            P(),
        ),
        out_specs=(P(EXPERT, "tensor"), P(EXPERT, "tensor")),
        check_vma=False,
    )
```

```python
import jax
import jax.numpy as jnp
from jax import lax
from jax.sharding import Mesh, PartitionSpec as P

D = 4096
MOST = 32


EPS = 1e-05


def finish_slots(gate_val, up_val, down_weight):
    active = (jax.nn.silu(gate_val) * up_val).astype(jnp.bfloat16)
    partial_out = jnp.einsum("gmf,fd->gmd", active, down_weight, preferred_element_type=jnp.float32)
    summed = lax.psum_scatter(
        partial_out.astype(jnp.bfloat16), "tensor", scatter_dimension=2, tiled=True
    )
    return lax.all_to_all(summed, EXPERT, split_axis=0, concat_axis=0, tiled=True)


def final_norm(stream, final_gain):
    stream_f = stream.astype(jnp.float32)
    square_total = lax.psum(jnp.sum(stream_f * stream_f, axis=1), "tensor")
    factor = lax.rsqrt(square_total / D + EPS)
    return (stream_f * factor[:, None] * final_gain).astype(jnp.bfloat16)


EXPERT = ("ex", "ez")


def restore(stream, row_order, source):
    outer = lax.axis_size("ex")
    inner = lax.axis_size("ez")
    rows = stream.shape[0]
    x_idx = lax.axis_index("ex")
    z_idx = lax.axis_index("ez")
    e_idx = x_idx * inner + z_idx
    gathered = lax.all_gather(stream, "ex", axis=0, tiled=True)
    dest = row_order // rows
    held = (
        (jnp.arange(outer, dtype=jnp.int32)[:, None] * inner + z_idx) * rows
        + jnp.arange(rows, dtype=jnp.int32)[None, :]
    ).reshape(-1)
    held_dest = jnp.take(dest, held, axis=0)
    count = held.shape[0]
    order = jnp.arange(count, dtype=jnp.int32)
    earlier = (held_dest[:, None] == held_dest[None, :]) & (order[None, :] < order[:, None])
    held_slot = jnp.sum(earlier.astype(jnp.int32), axis=1)
    mine = (held_dest // inner) == x_idx
    pick = (
        mine[None, None, :]
        & ((held_dest % inner)[None, None, :] == jnp.arange(inner, dtype=jnp.int32)[:, None, None])
        & (held_slot[None, None, :] == jnp.arange(rows, dtype=jnp.int32)[None, :, None])
    ).astype(jnp.bfloat16)
    send = jnp.einsum("zkg,gf->zkf", pick, gathered, preferred_element_type=jnp.float32).astype(
        jnp.bfloat16
    )
    received = lax.all_to_all(send, "ez", split_axis=0, concat_axis=0, tiled=True)
    arrival = jnp.arange(row_order.shape[0], dtype=jnp.int32)
    column = (arrival // rows) % inner
    source_column = (source // rows) % inner
    before = (
        (dest == e_idx)[None, :]
        & (column[None, :] == source_column[:, None])
        & (arrival[None, :] < source[:, None])
    )
    slot = jnp.sum(before.astype(jnp.int32), axis=1)
    flat = received.reshape(inner * rows, received.shape[2])
    return jnp.take(flat, source_column * rows + slot, axis=0)


def on_device(
    attn_vals,
    residual,
    out_weight,
    norm_gain,
    router_weight,
    routes,
    w_gate,
    w_up,
    w_down,
    slab_of,
    final_gain,
    row_order,
):
    groups = lax.axis_size("ex") * lax.axis_size("ez")
    row_count = attn_vals.shape[0]
    expert_count = router_weight.shape[1]
    slab_count = groups // expert_count
    partial_proj = jnp.dot(attn_vals, out_weight, preferred_element_type=jnp.float32)
    tensor_count = lax.axis_size("tensor")
    width = partial_proj.shape[1] // tensor_count
    pieces = partial_proj.astype(jnp.bfloat16).reshape(row_count, tensor_count, width)
    received = lax.all_to_all(
        pieces.transpose(1, 0, 2), "tensor", split_axis=0, concat_axis=0, tiled=True
    )
    project = jnp.sum(received.astype(jnp.float32), axis=0)
    stream_in = (residual.astype(jnp.float32) + project).astype(jnp.bfloat16)
    hidden_f = stream_in.astype(jnp.float32)
    scaled = hidden_f * norm_gain
    square_sum, logit_part = lax.psum(
        (
            jnp.sum(hidden_f * hidden_f, axis=1),
            jnp.dot(scaled, router_weight, precision=lax.Precision.HIGHEST),
        ),
        "tensor",
    )
    inverse_rms = lax.rsqrt(square_sum / D + EPS)
    normed_in = (scaled * inverse_rms[:, None]).astype(jnp.bfloat16)
    logits = logit_part * inverse_rms[:, None]
    expert_ids = jnp.arange(expert_count, dtype=jnp.int32)
    route_hot = (routes[:, :, None] == expert_ids[None, None, :]).astype(jnp.int32)
    chosen = jnp.sum(route_hot.astype(jnp.float32) * logits[:, None, :], axis=2)
    leading = jax.nn.sigmoid(chosen[:, 0] - chosen[:, 1])
    mixing = jnp.stack([leading, 1.0 - leading], axis=1)
    route_hits = jnp.sum(route_hot, axis=1)
    before_count = jnp.cumsum(route_hits, axis=0) - route_hits
    slot_ids = jnp.sum(route_hot * before_count[:, None, :], axis=2)
    slot_hot = (slot_ids[:, :, None] == jnp.arange(MOST, dtype=jnp.int32)[None, None, :]).astype(
        jnp.float32
    )
    placing = jnp.einsum("rke,rks->esr", route_hot.astype(jnp.float32), slot_hot).astype(
        jnp.bfloat16
    )
    target_expert = slab_of // slab_count
    send_map = jnp.take(placing, target_expert, axis=0)
    outgoing = jnp.einsum(
        "gsr,rd->gsd", send_map, normed_in, preferred_element_type=jnp.float32
    ).astype(jnp.bfloat16)
    arrived_part = lax.all_to_all(outgoing, EXPERT, split_axis=0, concat_axis=0, tiled=True)
    arrived = lax.all_gather(arrived_part, "tensor", axis=2, tiled=True)
    gate_val = jnp.einsum("gmd,df->gmf", arrived, w_gate[0], preferred_element_type=jnp.float32)
    up_val = jnp.einsum("gmd,df->gmf", arrived, w_up[0], preferred_element_type=jnp.float32)
    returned = finish_slots(gate_val, up_val, w_down[0])
    group_ids = jnp.arange(groups, dtype=jnp.int32)
    holder_hot = (slab_of[None, :] == group_ids[:, None]).astype(jnp.int32)
    holders = jnp.sum(holder_hot * group_ids[None, :], axis=1).reshape(expert_count, slab_count)
    row_holders = jnp.take(holders, routes, axis=0)
    flat_index = row_holders * MOST + slot_ids[:, :, None]
    flat_back = returned.reshape(groups * MOST, returned.shape[2])
    fetched = jnp.take(flat_back, flat_index.reshape(-1), axis=0).reshape(
        row_count, 2, slab_count, returned.shape[2]
    )
    expert_out = jnp.sum(fetched.astype(jnp.float32), axis=2)
    blended = jnp.sum(mixing[:, :, None] * expert_out, axis=1)
    stream = (hidden_f + blended).astype(jnp.bfloat16)
    positions = (lax.axis_index("ex") * lax.axis_size("ez") + lax.axis_index("ez")) * row_count + jnp.arange(row_count, dtype=jnp.int32)
    matches = (row_order[None, :] == positions[:, None]).astype(jnp.int32)
    source = jnp.sum(matches * jnp.arange(row_order.shape[0], dtype=jnp.int32)[None, :], axis=1)
    ordered = restore(stream, row_order, source)
    return (ordered, final_norm(ordered, final_gain))


def outer_size(mesh):
    column = mesh.devices[:, 0]
    try:
        outer = len({d.coords[0] for d in column})
    except AttributeError:
        outer = 1
    if outer < 1 or column.shape[0] % outer:
        outer = 1
    return outer


def solution(mesh):
    outer = outer_size(mesh)
    shape = mesh.devices.shape
    split = Mesh(mesh.devices.reshape(outer, shape[0] // outer, shape[1]), ("ex", "ez", "tensor"))
    return jax.shard_map(
        on_device,
        mesh=split,
        in_specs=(
            P(EXPERT, "tensor"),
            P(EXPERT, "tensor"),
            P("tensor", None),
            P("tensor"),
            P("tensor", None),
            P(EXPERT, None),
            P(EXPERT, None, "tensor"),
            P(EXPERT, None, "tensor"),
            P(EXPERT, "tensor", None),
            P(),
            P("tensor"),
            P(),
        ),
        out_specs=(P(EXPERT, "tensor"), P(EXPERT, "tensor")),
        check_vma=False,
    )
```

```python
import jax
import jax.numpy as jnp
from jax import lax
from jax.sharding import Mesh, PartitionSpec as P

D = 4096
MOST = 32


EPS = 1e-05


def finish_slots(gate_val, up_val, down_weight):
    active = (jax.nn.silu(gate_val) * up_val).astype(jnp.bfloat16)
    partial_out = jnp.einsum("gmf,fd->gmd", active, down_weight, preferred_element_type=jnp.float32)
    summed = lax.psum_scatter(
        partial_out.astype(jnp.bfloat16), "tensor", scatter_dimension=2, tiled=True
    )
    return lax.all_to_all(summed, EXPERT, split_axis=0, concat_axis=0, tiled=True)


def final_norm(stream, final_gain):
    stream_f = stream.astype(jnp.float32)
    square_total = lax.psum(jnp.sum(stream_f * stream_f, axis=1), "tensor")
    factor = lax.rsqrt(square_total / D + EPS)
    return (stream_f * factor[:, None] * final_gain).astype(jnp.bfloat16)


EXPERT = ("ex", "ez")


def restore(stream, row_order, source):
    outer = lax.axis_size("ex")
    inner = lax.axis_size("ez")
    rows = stream.shape[0]
    x_idx = lax.axis_index("ex")
    z_idx = lax.axis_index("ez")
    e_idx = x_idx * inner + z_idx
    gathered = lax.all_gather(stream, "ex", axis=0, tiled=True)
    dest = row_order // rows
    held = (
        (jnp.arange(outer, dtype=jnp.int32)[:, None] * inner + z_idx) * rows
        + jnp.arange(rows, dtype=jnp.int32)[None, :]
    ).reshape(-1)
    held_dest = jnp.take(dest, held, axis=0)
    count = held.shape[0]
    order = jnp.arange(count, dtype=jnp.int32)
    earlier = (held_dest[:, None] == held_dest[None, :]) & (order[None, :] < order[:, None])
    held_slot = jnp.sum(earlier.astype(jnp.int32), axis=1)
    mine = (held_dest // inner) == x_idx
    pick = (
        mine[None, None, :]
        & ((held_dest % inner)[None, None, :] == jnp.arange(inner, dtype=jnp.int32)[:, None, None])
        & (held_slot[None, None, :] == jnp.arange(rows, dtype=jnp.int32)[None, :, None])
    ).astype(jnp.bfloat16)
    send = jnp.einsum("zkg,gf->zkf", pick, gathered, preferred_element_type=jnp.float32).astype(
        jnp.bfloat16
    )
    received = lax.all_to_all(send, "ez", split_axis=0, concat_axis=0, tiled=True)
    arrival = jnp.arange(row_order.shape[0], dtype=jnp.int32)
    column = (arrival // rows) % inner
    source_column = (source // rows) % inner
    before = (
        (dest == e_idx)[None, :]
        & (column[None, :] == source_column[:, None])
        & (arrival[None, :] < source[:, None])
    )
    slot = jnp.sum(before.astype(jnp.int32), axis=1)
    flat = received.reshape(inner * rows, received.shape[2])
    return jnp.take(flat, source_column * rows + slot, axis=0)


def on_device(
    attn_vals,
    residual,
    out_weight,
    norm_gain,
    router_weight,
    routes,
    w_gate,
    w_up,
    w_down,
    slab_of,
    final_gain,
    row_order,
):
    groups = lax.axis_size("ex") * lax.axis_size("ez")
    row_count = attn_vals.shape[0]
    expert_count = router_weight.shape[1]
    slab_count = groups // expert_count
    partial_proj = jnp.dot(attn_vals, out_weight, preferred_element_type=jnp.float32)
    tensor_count = lax.axis_size("tensor")
    width = partial_proj.shape[1] // tensor_count
    pieces = partial_proj.astype(jnp.bfloat16).reshape(row_count, tensor_count, width)
    received = lax.all_to_all(
        pieces.transpose(1, 0, 2), "tensor", split_axis=0, concat_axis=0, tiled=True
    )
    project = jnp.sum(received.astype(jnp.float32), axis=0)
    stream_in = (residual.astype(jnp.float32) + project).astype(jnp.bfloat16)
    hidden_f = stream_in.astype(jnp.float32)
    scaled = hidden_f * norm_gain
    square_sum, logit_part = lax.psum(
        (
            jnp.sum(hidden_f * hidden_f, axis=1),
            jnp.dot(scaled, router_weight, precision=lax.Precision.HIGHEST),
        ),
        "tensor",
    )
    inverse_rms = lax.rsqrt(square_sum / D + EPS)
    logits = logit_part * inverse_rms[:, None]
    expert_ids = jnp.arange(expert_count, dtype=jnp.int32)
    route_hot = (routes[:, :, None] == expert_ids[None, None, :]).astype(jnp.int32)
    chosen = jnp.sum(route_hot.astype(jnp.float32) * logits[:, None, :], axis=2)
    leading = jax.nn.sigmoid(chosen[:, 0] - chosen[:, 1])
    mixing = jnp.stack([leading, 1.0 - leading], axis=1)
    route_hits = jnp.sum(route_hot, axis=1)
    before_count = jnp.cumsum(route_hits, axis=0) - route_hits
    slot_ids = jnp.sum(route_hot * before_count[:, None, :], axis=2)
    slot_hot = (slot_ids[:, :, None] == jnp.arange(MOST, dtype=jnp.int32)[None, None, :]).astype(
        jnp.float32
    )
    placing = jnp.einsum("rke,rks->esr", route_hot.astype(jnp.float32), slot_hot).astype(
        jnp.bfloat16
    )
    target_expert = slab_of // slab_count
    send_map = jnp.take(placing, target_expert, axis=0)
    outgoing = jnp.einsum(
        "gsr,rd->gsd", send_map, stream_in, preferred_element_type=jnp.float32
    ).astype(jnp.bfloat16)
    arrived_part = lax.all_to_all(outgoing, EXPERT, split_axis=0, concat_axis=0, tiled=True)
    arrived_rows = lax.all_gather(arrived_part, "tensor", axis=2, tiled=True).astype(jnp.float32)
    gain_full = lax.all_gather(norm_gain, "tensor", axis=0, tiled=True)
    slot_rms = lax.rsqrt(jnp.sum(arrived_rows * arrived_rows, axis=2) / D + EPS)
    arrived = (arrived_rows * gain_full * slot_rms[:, :, None]).astype(jnp.bfloat16)
    gate_val = jnp.einsum("gmd,df->gmf", arrived, w_gate[0], preferred_element_type=jnp.float32)
    up_val = jnp.einsum("gmd,df->gmf", arrived, w_up[0], preferred_element_type=jnp.float32)
    returned = finish_slots(gate_val, up_val, w_down[0])
    group_ids = jnp.arange(groups, dtype=jnp.int32)
    holder_hot = (slab_of[None, :] == group_ids[:, None]).astype(jnp.int32)
    holders = jnp.sum(holder_hot * group_ids[None, :], axis=1).reshape(expert_count, slab_count)
    row_holders = jnp.take(holders, routes, axis=0)
    flat_index = row_holders * MOST + slot_ids[:, :, None]
    flat_back = returned.reshape(groups * MOST, returned.shape[2])
    fetched = jnp.take(flat_back, flat_index.reshape(-1), axis=0).reshape(
        row_count, 2, slab_count, returned.shape[2]
    )
    expert_out = jnp.sum(fetched.astype(jnp.float32), axis=2)
    blended = jnp.sum(mixing[:, :, None] * expert_out, axis=1)
    stream = (hidden_f + blended).astype(jnp.bfloat16)
    positions = (lax.axis_index("ex") * lax.axis_size("ez") + lax.axis_index("ez")) * row_count + jnp.arange(row_count, dtype=jnp.int32)
    matches = (row_order[None, :] == positions[:, None]).astype(jnp.int32)
    source = jnp.sum(matches * jnp.arange(row_order.shape[0], dtype=jnp.int32)[None, :], axis=1)
    ordered = restore(stream, row_order, source)
    return (ordered, final_norm(ordered, final_gain))


def outer_size(mesh):
    column = mesh.devices[:, 0]
    try:
        outer = len({d.coords[0] for d in column})
    except AttributeError:
        outer = 1
    if outer < 1 or column.shape[0] % outer:
        outer = 1
    return outer


def solution(mesh):
    outer = outer_size(mesh)
    shape = mesh.devices.shape
    split = Mesh(mesh.devices.reshape(outer, shape[0] // outer, shape[1]), ("ex", "ez", "tensor"))
    return jax.shard_map(
        on_device,
        mesh=split,
        in_specs=(
            P(EXPERT, "tensor"),
            P(EXPERT, "tensor"),
            P("tensor", None),
            P("tensor"),
            P("tensor", None),
            P(EXPERT, None),
            P(EXPERT, None, "tensor"),
            P(EXPERT, None, "tensor"),
            P(EXPERT, "tensor", None),
            P(),
            P("tensor"),
            P(),
        ),
        out_specs=(P(EXPERT, "tensor"), P(EXPERT, "tensor")),
        check_vma=False,
    )
```

```python
import jax
import jax.numpy as jnp
from jax import lax
from jax.sharding import Mesh, PartitionSpec as P

D = 4096
MOST = 32


EPS = 1e-05


def finish_slots(gate_val, up_val, down_weight):
    active = (jax.nn.silu(gate_val) * up_val).astype(jnp.bfloat16)
    partial_out = jnp.einsum("gmf,fd->gmd", active, down_weight, preferred_element_type=jnp.float32)
    summed = lax.psum_scatter(
        partial_out.astype(jnp.bfloat16), "tensor", scatter_dimension=2, tiled=True
    )
    return lax.all_to_all(summed, EXPERT, split_axis=0, concat_axis=0, tiled=True)


def final_norm(stream, final_gain):
    stream_f = stream.astype(jnp.float32)
    square_total = lax.psum(jnp.sum(stream_f * stream_f, axis=1), "tensor")
    factor = lax.rsqrt(square_total / D + EPS)
    return (stream_f * factor[:, None] * final_gain).astype(jnp.bfloat16)


EXPERT = ("ex", "ez")


def restore(stream, row_order, source):
    outer = lax.axis_size("ex")
    inner = lax.axis_size("ez")
    rows = stream.shape[0]
    x_idx = lax.axis_index("ex")
    z_idx = lax.axis_index("ez")
    e_idx = x_idx * inner + z_idx
    gathered = lax.all_gather(stream, "ex", axis=0, tiled=True)
    dest = row_order // rows
    held = (
        (jnp.arange(outer, dtype=jnp.int32)[:, None] * inner + z_idx) * rows
        + jnp.arange(rows, dtype=jnp.int32)[None, :]
    ).reshape(-1)
    held_dest = jnp.take(dest, held, axis=0)
    count = held.shape[0]
    order = jnp.arange(count, dtype=jnp.int32)
    earlier = (held_dest[:, None] == held_dest[None, :]) & (order[None, :] < order[:, None])
    held_slot = jnp.sum(earlier.astype(jnp.int32), axis=1)
    mine = (held_dest // inner) == x_idx
    pick = (
        mine[None, None, :]
        & ((held_dest % inner)[None, None, :] == jnp.arange(inner, dtype=jnp.int32)[:, None, None])
        & (held_slot[None, None, :] == jnp.arange(rows, dtype=jnp.int32)[None, :, None])
    ).astype(jnp.bfloat16)
    send = jnp.einsum("zkg,gf->zkf", pick, gathered, preferred_element_type=jnp.float32).astype(
        jnp.bfloat16
    )
    received = lax.all_to_all(send, "ez", split_axis=0, concat_axis=0, tiled=True)
    arrival = jnp.arange(row_order.shape[0], dtype=jnp.int32)
    column = (arrival // rows) % inner
    source_column = (source // rows) % inner
    before = (
        (dest == e_idx)[None, :]
        & (column[None, :] == source_column[:, None])
        & (arrival[None, :] < source[:, None])
    )
    slot = jnp.sum(before.astype(jnp.int32), axis=1)
    flat = received.reshape(inner * rows, received.shape[2])
    return jnp.take(flat, source_column * rows + slot, axis=0)


def on_device(
    attn_vals,
    residual,
    out_weight,
    norm_gain,
    router_weight,
    routes,
    w_gate,
    w_up,
    w_down,
    slab_of,
    final_gain,
    row_order,
):
    groups = lax.axis_size("ex") * lax.axis_size("ez")
    row_count = attn_vals.shape[0]
    expert_count = router_weight.shape[1]
    slab_count = groups // expert_count
    partial_proj = jnp.dot(attn_vals, out_weight, preferred_element_type=jnp.float32)
    tensor_count = lax.axis_size("tensor")
    width = partial_proj.shape[1] // tensor_count
    pieces = partial_proj.astype(jnp.bfloat16).reshape(row_count, tensor_count, width)
    received = lax.all_to_all(
        pieces.transpose(1, 0, 2), "tensor", split_axis=0, concat_axis=0, tiled=True
    )
    project = jnp.sum(received.astype(jnp.float32), axis=0)
    stream_in = (residual.astype(jnp.float32) + project).astype(jnp.bfloat16)
    hidden_f = stream_in.astype(jnp.float32)
    scaled = hidden_f * norm_gain
    square_sum, logit_part = lax.psum(
        (
            jnp.sum(hidden_f * hidden_f, axis=1),
            jnp.dot(scaled, router_weight, precision=lax.Precision.HIGHEST),
        ),
        "tensor",
    )
    inverse_rms = lax.rsqrt(square_sum / D + EPS)
    logits = logit_part * inverse_rms[:, None]
    expert_ids = jnp.arange(expert_count, dtype=jnp.int32)
    route_hot = (routes[:, :, None] == expert_ids[None, None, :]).astype(jnp.int32)
    chosen = jnp.sum(route_hot.astype(jnp.float32) * logits[:, None, :], axis=2)
    leading = jax.nn.sigmoid(chosen[:, 0] - chosen[:, 1])
    mixing = jnp.stack([leading, 1.0 - leading], axis=1)
    route_hits = jnp.sum(route_hot, axis=1)
    before_count = jnp.cumsum(route_hits, axis=0) - route_hits
    slot_ids = jnp.sum(route_hot * before_count[:, None, :], axis=2)
    slot_hot = (slot_ids[:, :, None] == jnp.arange(MOST, dtype=jnp.int32)[None, None, :]).astype(
        jnp.float32
    )
    placing = jnp.einsum("rke,rks->esr", route_hot.astype(jnp.float32), slot_hot).astype(
        jnp.bfloat16
    )
    target_expert = slab_of // slab_count
    send_map = jnp.take(placing, target_expert, axis=0)
    outgoing = jnp.einsum(
        "gsr,rd->gsd", send_map, stream_in, preferred_element_type=jnp.float32
    ).astype(jnp.bfloat16)
    arrived_part = lax.all_to_all(outgoing, EXPERT, split_axis=0, concat_axis=0, tiled=True)
    arrived = lax.all_gather(arrived_part, "tensor", axis=2, tiled=True)
    arrived_f = arrived.astype(jnp.float32)
    slot_rms = lax.rsqrt(jnp.sum(arrived_f * arrived_f, axis=2) / D + EPS)[:, :, None]
    gain_full = lax.all_gather(norm_gain, "tensor", axis=0, tiled=True)[:, None]
    gate_weight = (w_gate[0].astype(jnp.float32) * gain_full).astype(jnp.bfloat16)
    up_weight = (w_up[0].astype(jnp.float32) * gain_full).astype(jnp.bfloat16)
    gate_val = slot_rms * jnp.einsum(
        "gmd,df->gmf", arrived, gate_weight, preferred_element_type=jnp.float32
    )
    up_val = slot_rms * jnp.einsum("gmd,df->gmf", arrived, up_weight, preferred_element_type=jnp.float32)
    returned = finish_slots(gate_val, up_val, w_down[0])
    group_ids = jnp.arange(groups, dtype=jnp.int32)
    holder_hot = (slab_of[None, :] == group_ids[:, None]).astype(jnp.int32)
    holders = jnp.sum(holder_hot * group_ids[None, :], axis=1).reshape(expert_count, slab_count)
    row_holders = jnp.take(holders, routes, axis=0)
    flat_index = row_holders * MOST + slot_ids[:, :, None]
    flat_back = returned.reshape(groups * MOST, returned.shape[2])
    fetched = jnp.take(flat_back, flat_index.reshape(-1), axis=0).reshape(
        row_count, 2, slab_count, returned.shape[2]
    )
    expert_out = jnp.sum(fetched.astype(jnp.float32), axis=2)
    blended = jnp.sum(mixing[:, :, None] * expert_out, axis=1)
    stream = (hidden_f + blended).astype(jnp.bfloat16)
    positions = (lax.axis_index("ex") * lax.axis_size("ez") + lax.axis_index("ez")) * row_count + jnp.arange(row_count, dtype=jnp.int32)
    matches = (row_order[None, :] == positions[:, None]).astype(jnp.int32)
    source = jnp.sum(matches * jnp.arange(row_order.shape[0], dtype=jnp.int32)[None, :], axis=1)
    ordered = restore(stream, row_order, source)
    return (ordered, final_norm(ordered, final_gain))


def outer_size(mesh):
    column = mesh.devices[:, 0]
    try:
        outer = len({d.coords[0] for d in column})
    except AttributeError:
        outer = 1
    if outer < 1 or column.shape[0] % outer:
        outer = 1
    return outer


def solution(mesh):
    outer = outer_size(mesh)
    shape = mesh.devices.shape
    split = Mesh(mesh.devices.reshape(outer, shape[0] // outer, shape[1]), ("ex", "ez", "tensor"))
    return jax.shard_map(
        on_device,
        mesh=split,
        in_specs=(
            P(EXPERT, "tensor"),
            P(EXPERT, "tensor"),
            P("tensor", None),
            P("tensor"),
            P("tensor", None),
            P(EXPERT, None),
            P(EXPERT, None, "tensor"),
            P(EXPERT, None, "tensor"),
            P(EXPERT, "tensor", None),
            P(),
            P("tensor"),
            P(),
        ),
        out_specs=(P(EXPERT, "tensor"), P(EXPERT, "tensor")),
        check_vma=False,
    )
```

```python
import jax
import jax.numpy as jnp
from jax import lax
from jax.sharding import Mesh, PartitionSpec as P

D = 4096
MOST = 32


EPS = 1e-05


def finish_slots(gate_val, up_val, down_weight):
    active = lax.optimization_barrier((jax.nn.silu(gate_val) * up_val).astype(jnp.bfloat16))
    partial_out = jnp.einsum("gmf,fd->gmd", active, down_weight, preferred_element_type=jnp.float32)
    summed = lax.psum_scatter(
        partial_out.astype(jnp.bfloat16), "tensor", scatter_dimension=2, tiled=True
    )
    return lax.all_to_all(summed, EXPERT, split_axis=0, concat_axis=0, tiled=True)


def final_norm(stream, final_gain):
    stream_f = stream.astype(jnp.float32)
    square_total = lax.psum(jnp.sum(stream_f * stream_f, axis=1), "tensor")
    factor = lax.rsqrt(square_total / D + EPS)
    return (stream_f * factor[:, None] * final_gain).astype(jnp.bfloat16)


EXPERT = ("ex", "ez")


def restore(stream, row_order, source):
    outer = lax.axis_size("ex")
    inner = lax.axis_size("ez")
    rows = stream.shape[0]
    x_idx = lax.axis_index("ex")
    z_idx = lax.axis_index("ez")
    e_idx = x_idx * inner + z_idx
    gathered = lax.all_gather(stream, "ex", axis=0, tiled=True)
    dest = row_order // rows
    held = (
        (jnp.arange(outer, dtype=jnp.int32)[:, None] * inner + z_idx) * rows
        + jnp.arange(rows, dtype=jnp.int32)[None, :]
    ).reshape(-1)
    held_dest = jnp.take(dest, held, axis=0)
    count = held.shape[0]
    order = jnp.arange(count, dtype=jnp.int32)
    earlier = (held_dest[:, None] == held_dest[None, :]) & (order[None, :] < order[:, None])
    held_slot = jnp.sum(earlier.astype(jnp.int32), axis=1)
    mine = (held_dest // inner) == x_idx
    pick = (
        mine[None, None, :]
        & ((held_dest % inner)[None, None, :] == jnp.arange(inner, dtype=jnp.int32)[:, None, None])
        & (held_slot[None, None, :] == jnp.arange(rows, dtype=jnp.int32)[None, :, None])
    ).astype(jnp.bfloat16)
    send = jnp.einsum("zkg,gf->zkf", pick, gathered, preferred_element_type=jnp.float32).astype(
        jnp.bfloat16
    )
    received = lax.all_to_all(send, "ez", split_axis=0, concat_axis=0, tiled=True)
    arrival = jnp.arange(row_order.shape[0], dtype=jnp.int32)
    column = (arrival // rows) % inner
    source_column = (source // rows) % inner
    before = (
        (dest == e_idx)[None, :]
        & (column[None, :] == source_column[:, None])
        & (arrival[None, :] < source[:, None])
    )
    slot = jnp.sum(before.astype(jnp.int32), axis=1)
    flat = received.reshape(inner * rows, received.shape[2])
    return jnp.take(flat, source_column * rows + slot, axis=0)


def on_device(
    attn_vals,
    residual,
    out_weight,
    norm_gain,
    router_weight,
    routes,
    w_gate,
    w_up,
    w_down,
    slab_of,
    final_gain,
    row_order,
):
    groups = lax.axis_size("ex") * lax.axis_size("ez")
    row_count = attn_vals.shape[0]
    expert_count = router_weight.shape[1]
    slab_count = groups // expert_count
    partial_proj = jnp.dot(attn_vals, out_weight, preferred_element_type=jnp.float32)
    tensor_count = lax.axis_size("tensor")
    width = partial_proj.shape[1] // tensor_count
    pieces = partial_proj.astype(jnp.bfloat16).reshape(row_count, tensor_count, width)
    received = lax.all_to_all(
        pieces.transpose(1, 0, 2), "tensor", split_axis=0, concat_axis=0, tiled=True
    )
    project = jnp.sum(received.astype(jnp.float32), axis=0)
    stream_in = (residual.astype(jnp.float32) + project).astype(jnp.bfloat16)
    hidden_f = stream_in.astype(jnp.float32)
    scaled = hidden_f * norm_gain
    square_sum, logit_part = lax.psum(
        (
            jnp.sum(hidden_f * hidden_f, axis=1),
            jnp.dot(scaled, router_weight, precision=lax.Precision.HIGHEST),
        ),
        "tensor",
    )
    inverse_rms = lax.rsqrt(square_sum / D + EPS)
    logits = logit_part * inverse_rms[:, None]
    expert_ids = jnp.arange(expert_count, dtype=jnp.int32)
    route_hot = (routes[:, :, None] == expert_ids[None, None, :]).astype(jnp.int32)
    chosen = jnp.sum(route_hot.astype(jnp.float32) * logits[:, None, :], axis=2)
    leading = jax.nn.sigmoid(chosen[:, 0] - chosen[:, 1])
    mixing = jnp.stack([leading, 1.0 - leading], axis=1)
    route_hits = jnp.sum(route_hot, axis=1)
    before_count = jnp.cumsum(route_hits, axis=0) - route_hits
    slot_ids = jnp.sum(route_hot * before_count[:, None, :], axis=2)
    slot_hot = (slot_ids[:, :, None] == jnp.arange(MOST, dtype=jnp.int32)[None, None, :]).astype(
        jnp.float32
    )
    placing = jnp.einsum("rke,rks->esr", route_hot.astype(jnp.float32), slot_hot).astype(
        jnp.bfloat16
    )
    target_expert = slab_of // slab_count
    send_map = jnp.take(placing, target_expert, axis=0)
    outgoing = jnp.einsum(
        "gsr,rd->gsd", send_map, stream_in, preferred_element_type=jnp.float32
    ).astype(jnp.bfloat16)
    arrived_part = lax.all_to_all(outgoing, EXPERT, split_axis=0, concat_axis=0, tiled=True)
    arrived = lax.all_gather(arrived_part, "tensor", axis=2, tiled=True)
    arrived_f = arrived.astype(jnp.float32)
    slot_rms = lax.rsqrt(jnp.sum(arrived_f * arrived_f, axis=2) / D + EPS)[:, :, None]
    gain_full = lax.all_gather(norm_gain, "tensor", axis=0, tiled=True)[:, None]
    gate_weight = (w_gate[0].astype(jnp.float32) * gain_full).astype(jnp.bfloat16)
    up_weight = (w_up[0].astype(jnp.float32) * gain_full).astype(jnp.bfloat16)
    gate_val = slot_rms * jnp.einsum(
        "gmd,df->gmf", arrived, gate_weight, preferred_element_type=jnp.float32
    )
    up_val = slot_rms * jnp.einsum("gmd,df->gmf", arrived, up_weight, preferred_element_type=jnp.float32)
    returned = finish_slots(gate_val, up_val, w_down[0])
    group_ids = jnp.arange(groups, dtype=jnp.int32)
    holder_hot = (slab_of[None, :] == group_ids[:, None]).astype(jnp.int32)
    holders = jnp.sum(holder_hot * group_ids[None, :], axis=1).reshape(expert_count, slab_count)
    row_holders = jnp.take(holders, routes, axis=0)
    flat_index = row_holders * MOST + slot_ids[:, :, None]
    flat_back = returned.reshape(groups * MOST, returned.shape[2])
    fetched = jnp.take(flat_back, flat_index.reshape(-1), axis=0).reshape(
        row_count, 2, slab_count, returned.shape[2]
    )
    expert_out = jnp.sum(fetched.astype(jnp.float32), axis=2)
    blended = jnp.sum(mixing[:, :, None] * expert_out, axis=1)
    stream = (hidden_f + blended).astype(jnp.bfloat16)
    positions = (lax.axis_index("ex") * lax.axis_size("ez") + lax.axis_index("ez")) * row_count + jnp.arange(row_count, dtype=jnp.int32)
    matches = (row_order[None, :] == positions[:, None]).astype(jnp.int32)
    source = jnp.sum(matches * jnp.arange(row_order.shape[0], dtype=jnp.int32)[None, :], axis=1)
    ordered = restore(stream, row_order, source)
    return (ordered, final_norm(ordered, final_gain))


def outer_size(mesh):
    column = mesh.devices[:, 0]
    try:
        outer = len({d.coords[0] for d in column})
    except AttributeError:
        outer = 1
    if outer < 1 or column.shape[0] % outer:
        outer = 1
    return outer


def solution(mesh):
    outer = outer_size(mesh)
    shape = mesh.devices.shape
    split = Mesh(mesh.devices.reshape(outer, shape[0] // outer, shape[1]), ("ex", "ez", "tensor"))
    return jax.shard_map(
        on_device,
        mesh=split,
        in_specs=(
            P(EXPERT, "tensor"),
            P(EXPERT, "tensor"),
            P("tensor", None),
            P("tensor"),
            P("tensor", None),
            P(EXPERT, None),
            P(EXPERT, None, "tensor"),
            P(EXPERT, None, "tensor"),
            P(EXPERT, "tensor", None),
            P(),
            P("tensor"),
            P(),
        ),
        out_specs=(P(EXPERT, "tensor"), P(EXPERT, "tensor")),
        check_vma=False,
    )
```

```python
import jax
import jax.numpy as jnp
from jax import lax
from jax.sharding import Mesh, PartitionSpec as P

D = 4096
MOST = 32


EPS = 1e-05


def finish_slots(gate_val, up_val, down_weight):
    active = lax.optimization_barrier((jax.nn.silu(gate_val) * up_val).astype(jnp.bfloat16))
    partial_out = jnp.einsum("gmf,fd->gmd", active, down_weight, preferred_element_type=jnp.float32)
    summed = lax.psum_scatter(
        partial_out.astype(jnp.bfloat16), "tensor", scatter_dimension=2, tiled=True
    )
    return lax.all_to_all(summed, EXPERT, split_axis=0, concat_axis=0, tiled=True)


def final_norm(stream, final_gain):
    stream_f = stream.astype(jnp.float32)
    square_total = lax.psum(jnp.sum(stream_f * stream_f, axis=1), "tensor")
    factor = lax.rsqrt(square_total / D + EPS)
    return (stream_f * factor[:, None] * final_gain).astype(jnp.bfloat16)


EXPERT = ("ex", "ez")


def restore(stream, row_order, source):
    outer = lax.axis_size("ex")
    inner = lax.axis_size("ez")
    rows = stream.shape[0]
    x_idx = lax.axis_index("ex")
    z_idx = lax.axis_index("ez")
    e_idx = x_idx * inner + z_idx
    gathered = lax.all_gather(stream, "ex", axis=0, tiled=True)
    dest = row_order // rows
    held = (
        (jnp.arange(outer, dtype=jnp.int32)[:, None] * inner + z_idx) * rows
        + jnp.arange(rows, dtype=jnp.int32)[None, :]
    ).reshape(-1)
    held_dest = jnp.take(dest, held, axis=0)
    count = held.shape[0]
    order = jnp.arange(count, dtype=jnp.int32)
    earlier = (held_dest[:, None] == held_dest[None, :]) & (order[None, :] < order[:, None])
    held_slot = jnp.sum(earlier.astype(jnp.int32), axis=1)
    mine = (held_dest // inner) == x_idx
    pick = (
        mine[None, None, :]
        & ((held_dest % inner)[None, None, :] == jnp.arange(inner, dtype=jnp.int32)[:, None, None])
        & (held_slot[None, None, :] == jnp.arange(rows, dtype=jnp.int32)[None, :, None])
    ).astype(jnp.bfloat16)
    send = jnp.einsum("zkg,gf->zkf", pick, gathered, preferred_element_type=jnp.float32).astype(
        jnp.bfloat16
    )
    received = lax.all_to_all(send, "ez", split_axis=0, concat_axis=0, tiled=True)
    arrival = jnp.arange(row_order.shape[0], dtype=jnp.int32)
    column = (arrival // rows) % inner
    source_column = (source // rows) % inner
    before = (
        (dest == e_idx)[None, :]
        & (column[None, :] == source_column[:, None])
        & (arrival[None, :] < source[:, None])
    )
    slot = jnp.sum(before.astype(jnp.int32), axis=1)
    flat = received.reshape(inner * rows, received.shape[2])
    return jnp.take(flat, source_column * rows + slot, axis=0)


def on_device(
    attn_vals,
    residual,
    out_weight,
    norm_gain,
    router_weight,
    routes,
    w_gate,
    w_up,
    w_down,
    slab_of,
    final_gain,
    row_order,
):
    groups = lax.axis_size("ex") * lax.axis_size("ez")
    row_count = attn_vals.shape[0]
    expert_count = router_weight.shape[1]
    slab_count = groups // expert_count
    partial_proj = jnp.dot(attn_vals, out_weight, preferred_element_type=jnp.float32)
    tensor_count = lax.axis_size("tensor")
    width = partial_proj.shape[1] // tensor_count
    pieces = partial_proj.astype(jnp.bfloat16).reshape(row_count, tensor_count, width)
    received = lax.all_to_all(
        pieces.transpose(1, 0, 2), "tensor", split_axis=0, concat_axis=0, tiled=True
    )
    project = jnp.sum(received.astype(jnp.float32), axis=0)
    stream_in = (residual.astype(jnp.float32) + project).astype(jnp.bfloat16)
    hidden_f = stream_in.astype(jnp.float32)
    scaled = hidden_f * norm_gain
    square_sum, logit_part = lax.psum(
        (
            jnp.sum(hidden_f * hidden_f, axis=1),
            jnp.dot(scaled, router_weight, precision=lax.Precision.HIGHEST),
        ),
        "tensor",
    )
    inverse_rms = lax.rsqrt(square_sum / D + EPS)
    logits = logit_part * inverse_rms[:, None]
    expert_ids = jnp.arange(expert_count, dtype=jnp.int32)
    route_hot = (routes[:, :, None] == expert_ids[None, None, :]).astype(jnp.int32)
    chosen = jnp.sum(route_hot.astype(jnp.float32) * logits[:, None, :], axis=2)
    leading = jax.nn.sigmoid(chosen[:, 0] - chosen[:, 1])
    mixing = jnp.stack([leading, 1.0 - leading], axis=1)
    route_hits = jnp.sum(route_hot, axis=1)
    before_count = jnp.cumsum(route_hits, axis=0) - route_hits
    slot_ids = jnp.sum(route_hot * before_count[:, None, :], axis=2)
    slot_hot = (slot_ids[:, :, None] == jnp.arange(MOST, dtype=jnp.int32)[None, None, :]).astype(
        jnp.float32
    )
    placing = jnp.einsum("rke,rks->esr", route_hot.astype(jnp.float32), slot_hot).astype(
        jnp.bfloat16
    )
    target_expert = slab_of // slab_count
    send_map = jnp.take(placing, target_expert, axis=0)
    outgoing = jnp.einsum(
        "gsr,rd->gsd", send_map, stream_in, preferred_element_type=jnp.float32
    ).astype(jnp.bfloat16)
    arrived_part = lax.all_to_all(outgoing, EXPERT, split_axis=0, concat_axis=0, tiled=True)
    arrived = lax.all_gather(arrived_part, "tensor", axis=2, tiled=True)
    part_f = arrived_part.astype(jnp.float32)
    slot_square = lax.psum(jnp.sum(part_f * part_f, axis=2), "tensor")
    slot_rms = lax.rsqrt(slot_square / D + EPS)[:, :, None]
    gain_full = lax.all_gather(norm_gain, "tensor", axis=0, tiled=True)[:, None]
    gate_weight = (w_gate[0].astype(jnp.float32) * gain_full).astype(jnp.bfloat16)
    up_weight = (w_up[0].astype(jnp.float32) * gain_full).astype(jnp.bfloat16)
    gate_val = slot_rms * jnp.einsum(
        "gmd,df->gmf", arrived, gate_weight, preferred_element_type=jnp.float32
    )
    up_val = slot_rms * jnp.einsum("gmd,df->gmf", arrived, up_weight, preferred_element_type=jnp.float32)
    returned = finish_slots(gate_val, up_val, w_down[0])
    group_ids = jnp.arange(groups, dtype=jnp.int32)
    holder_hot = (slab_of[None, :] == group_ids[:, None]).astype(jnp.int32)
    holders = jnp.sum(holder_hot * group_ids[None, :], axis=1).reshape(expert_count, slab_count)
    row_holders = jnp.take(holders, routes, axis=0)
    flat_index = row_holders * MOST + slot_ids[:, :, None]
    flat_back = returned.reshape(groups * MOST, returned.shape[2])
    fetched = jnp.take(flat_back, flat_index.reshape(-1), axis=0).reshape(
        row_count, 2, slab_count, returned.shape[2]
    )
    expert_out = jnp.sum(fetched.astype(jnp.float32), axis=2)
    blended = jnp.sum(mixing[:, :, None] * expert_out, axis=1)
    stream = (hidden_f + blended).astype(jnp.bfloat16)
    positions = (lax.axis_index("ex") * lax.axis_size("ez") + lax.axis_index("ez")) * row_count + jnp.arange(row_count, dtype=jnp.int32)
    matches = (row_order[None, :] == positions[:, None]).astype(jnp.int32)
    source = jnp.sum(matches * jnp.arange(row_order.shape[0], dtype=jnp.int32)[None, :], axis=1)
    ordered = restore(stream, row_order, source)
    return (ordered, final_norm(ordered, final_gain))


def outer_size(mesh):
    column = mesh.devices[:, 0]
    try:
        outer = len({d.coords[0] for d in column})
    except AttributeError:
        outer = 1
    if outer < 1 or column.shape[0] % outer:
        outer = 1
    return outer


def solution(mesh):
    outer = outer_size(mesh)
    shape = mesh.devices.shape
    split = Mesh(mesh.devices.reshape(outer, shape[0] // outer, shape[1]), ("ex", "ez", "tensor"))
    return jax.shard_map(
        on_device,
        mesh=split,
        in_specs=(
            P(EXPERT, "tensor"),
            P(EXPERT, "tensor"),
            P("tensor", None),
            P("tensor"),
            P("tensor", None),
            P(EXPERT, None),
            P(EXPERT, None, "tensor"),
            P(EXPERT, None, "tensor"),
            P(EXPERT, "tensor", None),
            P(),
            P("tensor"),
            P(),
        ),
        out_specs=(P(EXPERT, "tensor"), P(EXPERT, "tensor")),
        check_vma=False,
    )
```

```python
import jax
import jax.numpy as jnp
from jax import lax
from jax.sharding import Mesh, PartitionSpec as P

D = 4096
MOST = 32


EPS = 1e-05


def finish_slots(gate_val, up_val, down_weight):
    active = lax.optimization_barrier((jax.nn.silu(gate_val) * up_val).astype(jnp.bfloat16))
    partial_out = jnp.einsum("gmf,fd->gmd", active, down_weight, preferred_element_type=jnp.float32)
    summed = lax.psum_scatter(
        partial_out.astype(jnp.bfloat16), "tensor", scatter_dimension=2, tiled=True
    )
    return lax.all_to_all(summed, EXPERT, split_axis=0, concat_axis=0, tiled=True)


def final_norm(stream, final_gain):
    stream_f = stream.astype(jnp.float32)
    square_total = lax.psum(jnp.sum(stream_f * stream_f, axis=1), "tensor")
    factor = lax.rsqrt(square_total / D + EPS)
    return (stream_f * factor[:, None] * final_gain).astype(jnp.bfloat16)


EXPERT = ("ex", "ez")


def restore(stream, row_order, source):
    outer = lax.axis_size("ex")
    inner = lax.axis_size("ez")
    rows = stream.shape[0]
    x_idx = lax.axis_index("ex")
    z_idx = lax.axis_index("ez")
    e_idx = x_idx * inner + z_idx
    gathered = lax.all_gather(stream, "ez", axis=0, tiled=True)
    dest = row_order // rows
    held = (
        (x_idx * inner + jnp.arange(inner, dtype=jnp.int32)[:, None]) * rows
        + jnp.arange(rows, dtype=jnp.int32)[None, :]
    ).reshape(-1)
    held_dest = jnp.take(dest, held, axis=0)
    count = held.shape[0]
    order = jnp.arange(count, dtype=jnp.int32)
    earlier = (held_dest[:, None] == held_dest[None, :]) & (order[None, :] < order[:, None])
    held_slot = jnp.sum(earlier.astype(jnp.int32), axis=1)
    mine = (held_dest % inner) == z_idx
    pick = (
        mine[None, None, :]
        & ((held_dest // inner)[None, None, :] == jnp.arange(outer, dtype=jnp.int32)[:, None, None])
        & (held_slot[None, None, :] == jnp.arange(rows, dtype=jnp.int32)[None, :, None])
    ).astype(jnp.bfloat16)
    send = jnp.einsum("xkg,gf->xkf", pick, gathered, preferred_element_type=jnp.float32).astype(
        jnp.bfloat16
    )
    received = lax.all_to_all(send, "ex", split_axis=0, concat_axis=0, tiled=True)
    arrival = jnp.arange(row_order.shape[0], dtype=jnp.int32)
    column = arrival // (rows * inner)
    source_column = source // (rows * inner)
    before = (
        (dest == e_idx)[None, :]
        & (column[None, :] == source_column[:, None])
        & (arrival[None, :] < source[:, None])
    )
    slot = jnp.sum(before.astype(jnp.int32), axis=1)
    flat = received.reshape(outer * rows, received.shape[2])
    return jnp.take(flat, source_column * rows + slot, axis=0)


def on_device(
    attn_vals,
    residual,
    out_weight,
    norm_gain,
    router_weight,
    routes,
    w_gate,
    w_up,
    w_down,
    slab_of,
    final_gain,
    row_order,
):
    groups = lax.axis_size("ex") * lax.axis_size("ez")
    row_count = attn_vals.shape[0]
    expert_count = router_weight.shape[1]
    slab_count = groups // expert_count
    partial_proj = jnp.dot(attn_vals, out_weight, preferred_element_type=jnp.float32)
    tensor_count = lax.axis_size("tensor")
    width = partial_proj.shape[1] // tensor_count
    pieces = partial_proj.astype(jnp.bfloat16).reshape(row_count, tensor_count, width)
    received = lax.all_to_all(
        pieces.transpose(1, 0, 2), "tensor", split_axis=0, concat_axis=0, tiled=True
    )
    project = jnp.sum(received.astype(jnp.float32), axis=0)
    stream_in = (residual.astype(jnp.float32) + project).astype(jnp.bfloat16)
    hidden_f = stream_in.astype(jnp.float32)
    scaled = hidden_f * norm_gain
    square_sum, logit_part = lax.psum(
        (
            jnp.sum(hidden_f * hidden_f, axis=1),
            jnp.dot(scaled, router_weight, precision=lax.Precision.HIGHEST),
        ),
        "tensor",
    )
    inverse_rms = lax.rsqrt(square_sum / D + EPS)
    logits = logit_part * inverse_rms[:, None]
    expert_ids = jnp.arange(expert_count, dtype=jnp.int32)
    route_hot = (routes[:, :, None] == expert_ids[None, None, :]).astype(jnp.int32)
    chosen = jnp.sum(route_hot.astype(jnp.float32) * logits[:, None, :], axis=2)
    leading = jax.nn.sigmoid(chosen[:, 0] - chosen[:, 1])
    mixing = jnp.stack([leading, 1.0 - leading], axis=1)
    route_hits = jnp.sum(route_hot, axis=1)
    before_count = jnp.cumsum(route_hits, axis=0) - route_hits
    slot_ids = jnp.sum(route_hot * before_count[:, None, :], axis=2)
    slot_hot = (slot_ids[:, :, None] == jnp.arange(MOST, dtype=jnp.int32)[None, None, :]).astype(
        jnp.float32
    )
    placing = jnp.einsum("rke,rks->esr", route_hot.astype(jnp.float32), slot_hot).astype(
        jnp.bfloat16
    )
    target_expert = slab_of // slab_count
    send_map = jnp.take(placing, target_expert, axis=0)
    outgoing = jnp.einsum(
        "gsr,rd->gsd", send_map, stream_in, preferred_element_type=jnp.float32
    ).astype(jnp.bfloat16)
    arrived_part = lax.all_to_all(outgoing, EXPERT, split_axis=0, concat_axis=0, tiled=True)
    arrived = lax.all_gather(arrived_part, "tensor", axis=2, tiled=True)
    part_f = arrived_part.astype(jnp.float32)
    slot_square = lax.psum(jnp.sum(part_f * part_f, axis=2), "tensor")
    slot_rms = lax.rsqrt(slot_square / D + EPS)[:, :, None]
    gain_full = lax.all_gather(norm_gain, "tensor", axis=0, tiled=True)[:, None]
    gate_weight = (w_gate[0].astype(jnp.float32) * gain_full).astype(jnp.bfloat16)
    up_weight = (w_up[0].astype(jnp.float32) * gain_full).astype(jnp.bfloat16)
    gate_val = slot_rms * jnp.einsum(
        "gmd,df->gmf", arrived, gate_weight, preferred_element_type=jnp.float32
    )
    up_val = slot_rms * jnp.einsum("gmd,df->gmf", arrived, up_weight, preferred_element_type=jnp.float32)
    returned = finish_slots(gate_val, up_val, w_down[0])
    group_ids = jnp.arange(groups, dtype=jnp.int32)
    holder_hot = (slab_of[None, :] == group_ids[:, None]).astype(jnp.int32)
    holders = jnp.sum(holder_hot * group_ids[None, :], axis=1).reshape(expert_count, slab_count)
    row_holders = jnp.take(holders, routes, axis=0)
    flat_index = row_holders * MOST + slot_ids[:, :, None]
    flat_back = returned.reshape(groups * MOST, returned.shape[2])
    fetched = jnp.take(flat_back, flat_index.reshape(-1), axis=0).reshape(
        row_count, 2, slab_count, returned.shape[2]
    )
    expert_out = jnp.sum(fetched.astype(jnp.float32), axis=2)
    blended = jnp.sum(mixing[:, :, None] * expert_out, axis=1)
    stream = (hidden_f + blended).astype(jnp.bfloat16)
    positions = (lax.axis_index("ex") * lax.axis_size("ez") + lax.axis_index("ez")) * row_count + jnp.arange(row_count, dtype=jnp.int32)
    matches = (row_order[None, :] == positions[:, None]).astype(jnp.int32)
    source = jnp.sum(matches * jnp.arange(row_order.shape[0], dtype=jnp.int32)[None, :], axis=1)
    ordered = restore(stream, row_order, source)
    return (ordered, final_norm(ordered, final_gain))


def outer_size(mesh):
    column = mesh.devices[:, 0]
    try:
        outer = len({d.coords[0] for d in column})
    except AttributeError:
        outer = 1
    if outer < 1 or column.shape[0] % outer:
        outer = 1
    return outer


def solution(mesh):
    outer = outer_size(mesh)
    shape = mesh.devices.shape
    split = Mesh(mesh.devices.reshape(outer, shape[0] // outer, shape[1]), ("ex", "ez", "tensor"))
    return jax.shard_map(
        on_device,
        mesh=split,
        in_specs=(
            P(EXPERT, "tensor"),
            P(EXPERT, "tensor"),
            P("tensor", None),
            P("tensor"),
            P("tensor", None),
            P(EXPERT, None),
            P(EXPERT, None, "tensor"),
            P(EXPERT, None, "tensor"),
            P(EXPERT, "tensor", None),
            P(),
            P("tensor"),
            P(),
        ),
        out_specs=(P(EXPERT, "tensor"), P(EXPERT, "tensor")),
        check_vma=False,
    )
```

```python
import jax
import jax.numpy as jnp
from jax import lax
from jax.sharding import Mesh, PartitionSpec as P

D = 4096
MOST = 32


EPS = 1e-05


def finish_slots(gate_val, up_val, down_weight):
    active = lax.optimization_barrier((jax.nn.silu(gate_val) * up_val).astype(jnp.bfloat16))
    partial_out = jnp.einsum("gmf,fd->gmd", active, down_weight, preferred_element_type=jnp.float32)
    summed = lax.psum_scatter(
        partial_out.astype(jnp.bfloat16), "tensor", scatter_dimension=2, tiled=True
    )
    return lax.all_to_all(summed, EXPERT, split_axis=0, concat_axis=0, tiled=True)


def final_norm(stream, final_gain):
    stream_f = stream.astype(jnp.float32)
    square_total = lax.psum(jnp.sum(stream_f * stream_f, axis=1), "tensor")
    factor = lax.rsqrt(square_total / D + EPS)
    return (stream_f * factor[:, None] * final_gain).astype(jnp.bfloat16)


EXPERT = ("ex", "ez")


def restore(stream, row_order, source):
    outer = lax.axis_size("ex")
    inner = lax.axis_size("ez")
    rows = stream.shape[0]
    x_idx = lax.axis_index("ex")
    z_idx = lax.axis_index("ez")
    e_idx = x_idx * inner + z_idx
    gathered = lax.all_gather(stream, "ex", axis=0, tiled=True)
    dest = row_order // rows
    held = (
        (jnp.arange(outer, dtype=jnp.int32)[:, None] * inner + z_idx) * rows
        + jnp.arange(rows, dtype=jnp.int32)[None, :]
    ).reshape(-1)
    held_dest = jnp.take(dest, held, axis=0)
    count = held.shape[0]
    order = jnp.arange(count, dtype=jnp.int32)
    earlier = (held_dest[:, None] == held_dest[None, :]) & (order[None, :] < order[:, None])
    held_slot = jnp.sum(earlier.astype(jnp.int32), axis=1)
    mine = (held_dest // inner) == x_idx
    pick = (
        mine[None, None, :]
        & ((held_dest % inner)[None, None, :] == jnp.arange(inner, dtype=jnp.int32)[:, None, None])
        & (held_slot[None, None, :] == jnp.arange(rows, dtype=jnp.int32)[None, :, None])
    ).astype(jnp.bfloat16)
    send = jnp.einsum("zkg,gf->zkf", pick, gathered, preferred_element_type=jnp.float32).astype(
        jnp.bfloat16
    )
    received = lax.all_to_all(send, "ez", split_axis=0, concat_axis=0, tiled=True)
    arrival = jnp.arange(row_order.shape[0], dtype=jnp.int32)
    column = (arrival // rows) % inner
    source_column = (source // rows) % inner
    before = (
        (dest == e_idx)[None, :]
        & (column[None, :] == source_column[:, None])
        & (arrival[None, :] < source[:, None])
    )
    slot = jnp.sum(before.astype(jnp.int32), axis=1)
    flat = received.reshape(inner * rows, received.shape[2])
    return jnp.take(flat, source_column * rows + slot, axis=0)


def on_device(
    attn_vals,
    residual,
    out_weight,
    norm_gain,
    router_weight,
    routes,
    w_gate,
    w_up,
    w_down,
    slab_of,
    final_gain,
    row_order,
):
    groups = lax.axis_size("ex") * lax.axis_size("ez")
    row_count = attn_vals.shape[0]
    expert_count = router_weight.shape[1]
    slab_count = groups // expert_count
    partial_proj = jnp.dot(attn_vals, out_weight, preferred_element_type=jnp.float32)
    tensor_count = lax.axis_size("tensor")
    width = partial_proj.shape[1] // tensor_count
    pieces = partial_proj.astype(jnp.bfloat16).reshape(row_count, tensor_count, width)
    received = lax.all_to_all(
        pieces.transpose(1, 0, 2), "tensor", split_axis=0, concat_axis=0, tiled=True
    )
    project = jnp.sum(received.astype(jnp.float32), axis=0)
    stream_in = (residual.astype(jnp.float32) + project).astype(jnp.bfloat16)
    hidden_f = stream_in.astype(jnp.float32)
    scaled = hidden_f * norm_gain
    square_sum, logit_part = lax.psum(
        (
            jnp.sum(hidden_f * hidden_f, axis=1),
            jnp.dot(scaled, router_weight, precision=lax.Precision.HIGHEST),
        ),
        "tensor",
    )
    inverse_rms = lax.rsqrt(square_sum / D + EPS)
    logits = logit_part * inverse_rms[:, None]
    expert_ids = jnp.arange(expert_count, dtype=jnp.int32)
    route_hot = (routes[:, :, None] == expert_ids[None, None, :]).astype(jnp.int32)
    chosen = jnp.sum(route_hot.astype(jnp.float32) * logits[:, None, :], axis=2)
    leading = jax.nn.sigmoid(chosen[:, 0] - chosen[:, 1])
    mixing = jnp.stack([leading, 1.0 - leading], axis=1)
    route_hits = jnp.sum(route_hot, axis=1)
    before_count = jnp.cumsum(route_hits, axis=0) - route_hits
    slot_ids = jnp.sum(route_hot * before_count[:, None, :], axis=2)
    slot_hot = (slot_ids[:, :, None] == jnp.arange(MOST, dtype=jnp.int32)[None, None, :]).astype(
        jnp.float32
    )
    placing = jnp.einsum("rke,rks->esr", route_hot.astype(jnp.float32), slot_hot).astype(
        jnp.bfloat16
    )
    target_expert = slab_of // slab_count
    send_map = jnp.take(placing, target_expert, axis=0)
    outgoing = jnp.einsum(
        "gsr,rd->gsd", send_map, stream_in, preferred_element_type=jnp.float32
    ).astype(jnp.bfloat16)
    arrived_part = lax.all_to_all(outgoing, EXPERT, split_axis=0, concat_axis=0, tiled=True)
    part_f = arrived_part.astype(jnp.float32)
    arrived = lax.all_gather((part_f * norm_gain).astype(jnp.bfloat16), "tensor", axis=2, tiled=True)
    slot_square = lax.psum(jnp.sum(part_f * part_f, axis=2), "tensor")
    slot_rms = lax.rsqrt(slot_square / D + EPS)[:, :, None]
    gate_weight = w_gate[0]
    up_weight = w_up[0]
    gate_val = slot_rms * jnp.einsum(
        "gmd,df->gmf", arrived, gate_weight, preferred_element_type=jnp.float32
    )
    up_val = slot_rms * jnp.einsum("gmd,df->gmf", arrived, up_weight, preferred_element_type=jnp.float32)
    returned = finish_slots(gate_val, up_val, w_down[0])
    group_ids = jnp.arange(groups, dtype=jnp.int32)
    holder_hot = (slab_of[None, :] == group_ids[:, None]).astype(jnp.int32)
    holders = jnp.sum(holder_hot * group_ids[None, :], axis=1).reshape(expert_count, slab_count)
    row_holders = jnp.take(holders, routes, axis=0)
    flat_index = row_holders * MOST + slot_ids[:, :, None]
    flat_back = returned.reshape(groups * MOST, returned.shape[2])
    fetched = jnp.take(flat_back, flat_index.reshape(-1), axis=0).reshape(
        row_count, 2, slab_count, returned.shape[2]
    )
    expert_out = jnp.sum(fetched.astype(jnp.float32), axis=2)
    blended = jnp.sum(mixing[:, :, None] * expert_out, axis=1)
    stream = (hidden_f + blended).astype(jnp.bfloat16)
    positions = (lax.axis_index("ex") * lax.axis_size("ez") + lax.axis_index("ez")) * row_count + jnp.arange(row_count, dtype=jnp.int32)
    matches = (row_order[None, :] == positions[:, None]).astype(jnp.int32)
    source = jnp.sum(matches * jnp.arange(row_order.shape[0], dtype=jnp.int32)[None, :], axis=1)
    ordered = restore(stream, row_order, source)
    return (ordered, final_norm(ordered, final_gain))


def outer_size(mesh):
    column = mesh.devices[:, 0]
    try:
        outer = len({d.coords[0] for d in column})
    except AttributeError:
        outer = 1
    if outer < 1 or column.shape[0] % outer:
        outer = 1
    return outer


def solution(mesh):
    outer = outer_size(mesh)
    shape = mesh.devices.shape
    split = Mesh(mesh.devices.reshape(outer, shape[0] // outer, shape[1]), ("ex", "ez", "tensor"))
    return jax.shard_map(
        on_device,
        mesh=split,
        in_specs=(
            P(EXPERT, "tensor"),
            P(EXPERT, "tensor"),
            P("tensor", None),
            P("tensor"),
            P("tensor", None),
            P(EXPERT, None),
            P(EXPERT, None, "tensor"),
            P(EXPERT, None, "tensor"),
            P(EXPERT, "tensor", None),
            P(),
            P("tensor"),
            P(),
        ),
        out_specs=(P(EXPERT, "tensor"), P(EXPERT, "tensor")),
        check_vma=False,
    )
```

```python
import jax
import jax.numpy as jnp
from jax import lax
from jax.sharding import Mesh, PartitionSpec as P

D = 4096
MOST = 32


EPS = 1e-05


def finish_slots(gate_val, up_val, down_weight):
    active = lax.optimization_barrier((jax.nn.silu(gate_val) * up_val).astype(jnp.bfloat16))
    partial_out = jnp.einsum("gmf,fd->gmd", active, down_weight, preferred_element_type=jnp.float32)
    summed = lax.psum_scatter(
        partial_out.astype(jnp.bfloat16), "tensor", scatter_dimension=2, tiled=True
    )
    return lax.all_to_all(summed, EXPERT, split_axis=0, concat_axis=0, tiled=True)


def final_norm(stream, final_gain):
    stream_f = stream.astype(jnp.float32)
    square_total = lax.psum(jnp.sum(stream_f * stream_f, axis=1), "tensor")
    factor = lax.rsqrt(square_total / D + EPS)
    return (stream_f * factor[:, None] * final_gain).astype(jnp.bfloat16)


EXPERT = ("ex", "ez")


def restore(stream, row_order, source):
    outer = lax.axis_size("ex")
    inner = lax.axis_size("ez")
    rows = stream.shape[0]
    x_idx = lax.axis_index("ex")
    z_idx = lax.axis_index("ez")
    e_idx = x_idx * inner + z_idx
    copies = jnp.broadcast_to(stream[None], (outer,) + stream.shape)
    gathered = lax.all_to_all(copies, "ex", split_axis=0, concat_axis=0, tiled=True).reshape(
        outer * rows, stream.shape[1]
    )
    dest = row_order // rows
    held = (
        (jnp.arange(outer, dtype=jnp.int32)[:, None] * inner + z_idx) * rows
        + jnp.arange(rows, dtype=jnp.int32)[None, :]
    ).reshape(-1)
    held_dest = jnp.take(dest, held, axis=0)
    count = held.shape[0]
    order = jnp.arange(count, dtype=jnp.int32)
    earlier = (held_dest[:, None] == held_dest[None, :]) & (order[None, :] < order[:, None])
    held_slot = jnp.sum(earlier.astype(jnp.int32), axis=1)
    mine = (held_dest // inner) == x_idx
    pick = (
        mine[None, None, :]
        & ((held_dest % inner)[None, None, :] == jnp.arange(inner, dtype=jnp.int32)[:, None, None])
        & (held_slot[None, None, :] == jnp.arange(rows, dtype=jnp.int32)[None, :, None])
    ).astype(jnp.bfloat16)
    send = jnp.einsum("zkg,gf->zkf", pick, gathered, preferred_element_type=jnp.float32).astype(
        jnp.bfloat16
    )
    received = lax.all_to_all(send, "ez", split_axis=0, concat_axis=0, tiled=True)
    arrival = jnp.arange(row_order.shape[0], dtype=jnp.int32)
    column = (arrival // rows) % inner
    source_column = (source // rows) % inner
    before = (
        (dest == e_idx)[None, :]
        & (column[None, :] == source_column[:, None])
        & (arrival[None, :] < source[:, None])
    )
    slot = jnp.sum(before.astype(jnp.int32), axis=1)
    flat = received.reshape(inner * rows, received.shape[2])
    return jnp.take(flat, source_column * rows + slot, axis=0)


def on_device(
    attn_vals,
    residual,
    out_weight,
    norm_gain,
    router_weight,
    routes,
    w_gate,
    w_up,
    w_down,
    slab_of,
    final_gain,
    row_order,
):
    groups = lax.axis_size("ex") * lax.axis_size("ez")
    row_count = attn_vals.shape[0]
    expert_count = router_weight.shape[1]
    slab_count = groups // expert_count
    partial_proj = jnp.dot(attn_vals, out_weight, preferred_element_type=jnp.float32)
    tensor_count = lax.axis_size("tensor")
    width = partial_proj.shape[1] // tensor_count
    pieces = partial_proj.astype(jnp.bfloat16).reshape(row_count, tensor_count, width)
    received = lax.all_to_all(
        pieces.transpose(1, 0, 2), "tensor", split_axis=0, concat_axis=0, tiled=True
    )
    project = jnp.sum(received.astype(jnp.float32), axis=0)
    stream_in = (residual.astype(jnp.float32) + project).astype(jnp.bfloat16)
    hidden_f = stream_in.astype(jnp.float32)
    scaled = hidden_f * norm_gain
    square_sum, logit_part = lax.psum(
        (
            jnp.sum(hidden_f * hidden_f, axis=1),
            jnp.dot(scaled, router_weight, precision=lax.Precision.HIGHEST),
        ),
        "tensor",
    )
    inverse_rms = lax.rsqrt(square_sum / D + EPS)
    logits = logit_part * inverse_rms[:, None]
    expert_ids = jnp.arange(expert_count, dtype=jnp.int32)
    route_hot = (routes[:, :, None] == expert_ids[None, None, :]).astype(jnp.int32)
    chosen = jnp.sum(route_hot.astype(jnp.float32) * logits[:, None, :], axis=2)
    leading = jax.nn.sigmoid(chosen[:, 0] - chosen[:, 1])
    mixing = jnp.stack([leading, 1.0 - leading], axis=1)
    route_hits = jnp.sum(route_hot, axis=1)
    before_count = jnp.cumsum(route_hits, axis=0) - route_hits
    slot_ids = jnp.sum(route_hot * before_count[:, None, :], axis=2)
    slot_hot = (slot_ids[:, :, None] == jnp.arange(MOST, dtype=jnp.int32)[None, None, :]).astype(
        jnp.float32
    )
    placing = jnp.einsum("rke,rks->esr", route_hot.astype(jnp.float32), slot_hot).astype(
        jnp.bfloat16
    )
    target_expert = slab_of // slab_count
    send_map = jnp.take(placing, target_expert, axis=0)
    outgoing = jnp.einsum(
        "gsr,rd->gsd", send_map, stream_in, preferred_element_type=jnp.float32
    ).astype(jnp.bfloat16)
    arrived_part = lax.all_to_all(outgoing, EXPERT, split_axis=0, concat_axis=0, tiled=True)
    arrived = lax.all_gather(arrived_part, "tensor", axis=2, tiled=True)
    part_f = arrived_part.astype(jnp.float32)
    slot_square = lax.psum(jnp.sum(part_f * part_f, axis=2), "tensor")
    slot_rms = lax.rsqrt(slot_square / D + EPS)[:, :, None]
    gain_full = lax.all_gather(norm_gain, "tensor", axis=0, tiled=True)[:, None]
    gate_weight = (w_gate[0].astype(jnp.float32) * gain_full).astype(jnp.bfloat16)
    up_weight = (w_up[0].astype(jnp.float32) * gain_full).astype(jnp.bfloat16)
    gate_val = slot_rms * jnp.einsum(
        "gmd,df->gmf", arrived, gate_weight, preferred_element_type=jnp.float32
    )
    up_val = slot_rms * jnp.einsum("gmd,df->gmf", arrived, up_weight, preferred_element_type=jnp.float32)
    returned = finish_slots(gate_val, up_val, w_down[0])
    group_ids = jnp.arange(groups, dtype=jnp.int32)
    holder_hot = (slab_of[None, :] == group_ids[:, None]).astype(jnp.int32)
    holders = jnp.sum(holder_hot * group_ids[None, :], axis=1).reshape(expert_count, slab_count)
    row_holders = jnp.take(holders, routes, axis=0)
    flat_index = row_holders * MOST + slot_ids[:, :, None]
    flat_back = returned.reshape(groups * MOST, returned.shape[2])
    fetched = jnp.take(flat_back, flat_index.reshape(-1), axis=0).reshape(
        row_count, 2, slab_count, returned.shape[2]
    )
    expert_out = jnp.sum(fetched.astype(jnp.float32), axis=2)
    blended = jnp.sum(mixing[:, :, None] * expert_out, axis=1)
    stream = (hidden_f + blended).astype(jnp.bfloat16)
    positions = (lax.axis_index("ex") * lax.axis_size("ez") + lax.axis_index("ez")) * row_count + jnp.arange(row_count, dtype=jnp.int32)
    matches = (row_order[None, :] == positions[:, None]).astype(jnp.int32)
    source = jnp.sum(matches * jnp.arange(row_order.shape[0], dtype=jnp.int32)[None, :], axis=1)
    ordered = restore(stream, row_order, source)
    return (ordered, final_norm(ordered, final_gain))


def outer_size(mesh):
    column = mesh.devices[:, 0]
    try:
        outer = len({d.coords[0] for d in column})
    except AttributeError:
        outer = 1
    if outer < 1 or column.shape[0] % outer:
        outer = 1
    return outer


def solution(mesh):
    outer = outer_size(mesh)
    shape = mesh.devices.shape
    split = Mesh(mesh.devices.reshape(outer, shape[0] // outer, shape[1]), ("ex", "ez", "tensor"))
    return jax.shard_map(
        on_device,
        mesh=split,
        in_specs=(
            P(EXPERT, "tensor"),
            P(EXPERT, "tensor"),
            P("tensor", None),
            P("tensor"),
            P("tensor", None),
            P(EXPERT, None),
            P(EXPERT, None, "tensor"),
            P(EXPERT, None, "tensor"),
            P(EXPERT, "tensor", None),
            P(),
            P("tensor"),
            P(),
        ),
        out_specs=(P(EXPERT, "tensor"), P(EXPERT, "tensor")),
        check_vma=False,
    )
```

```python
import jax
import jax.numpy as jnp
from jax import lax
from jax.sharding import Mesh, PartitionSpec as P

D = 4096
MOST = 32


EPS = 1e-05


def finish_slots(gate_val, up_val, down_weight):
    active = lax.optimization_barrier((jax.nn.silu(gate_val) * up_val).astype(jnp.bfloat16))
    partial_out = jnp.einsum("gmf,fd->gmd", active, down_weight, preferred_element_type=jnp.float32)
    summed = lax.psum_scatter(
        partial_out.astype(jnp.bfloat16), "tensor", scatter_dimension=2, tiled=True
    )
    return lax.all_to_all(summed, EXPERT, split_axis=0, concat_axis=0, tiled=True)


def final_norm(stream, final_gain):
    stream_f = stream.astype(jnp.float32)
    square_total = jnp.sum(stream_f * stream_f, axis=1)
    count = lax.axis_size("tensor")
    step = 1
    while step < count:
        square_total = square_total + lax.ppermute(
            square_total, "tensor", [(i, i ^ step) for i in range(count)]
        )
        step *= 2
    factor = lax.rsqrt(square_total / D + EPS)
    return (stream_f * factor[:, None] * final_gain).astype(jnp.bfloat16)


EXPERT = ("ex", "ez")


def restore(stream, row_order, source):
    outer = lax.axis_size("ex")
    inner = lax.axis_size("ez")
    rows = stream.shape[0]
    x_idx = lax.axis_index("ex")
    z_idx = lax.axis_index("ez")
    e_idx = x_idx * inner + z_idx
    copies = jnp.broadcast_to(stream[None], (outer,) + stream.shape)
    gathered = lax.all_to_all(copies, "ex", split_axis=0, concat_axis=0, tiled=True).reshape(
        outer * rows, stream.shape[1]
    )
    dest = row_order // rows
    held = (
        (jnp.arange(outer, dtype=jnp.int32)[:, None] * inner + z_idx) * rows
        + jnp.arange(rows, dtype=jnp.int32)[None, :]
    ).reshape(-1)
    held_dest = jnp.take(dest, held, axis=0)
    count = held.shape[0]
    order = jnp.arange(count, dtype=jnp.int32)
    earlier = (held_dest[:, None] == held_dest[None, :]) & (order[None, :] < order[:, None])
    held_slot = jnp.sum(earlier.astype(jnp.int32), axis=1)
    mine = (held_dest // inner) == x_idx
    pick = (
        mine[None, None, :]
        & ((held_dest % inner)[None, None, :] == jnp.arange(inner, dtype=jnp.int32)[:, None, None])
        & (held_slot[None, None, :] == jnp.arange(rows, dtype=jnp.int32)[None, :, None])
    ).astype(jnp.bfloat16)
    send = jnp.einsum("zkg,gf->zkf", pick, gathered, preferred_element_type=jnp.float32).astype(
        jnp.bfloat16
    )
    received = lax.all_to_all(send, "ez", split_axis=0, concat_axis=0, tiled=True)
    arrival = jnp.arange(row_order.shape[0], dtype=jnp.int32)
    column = (arrival // rows) % inner
    source_column = (source // rows) % inner
    before = (
        (dest == e_idx)[None, :]
        & (column[None, :] == source_column[:, None])
        & (arrival[None, :] < source[:, None])
    )
    slot = jnp.sum(before.astype(jnp.int32), axis=1)
    flat = received.reshape(inner * rows, received.shape[2])
    return jnp.take(flat, source_column * rows + slot, axis=0)


def on_device(
    attn_vals,
    residual,
    out_weight,
    norm_gain,
    router_weight,
    routes,
    w_gate,
    w_up,
    w_down,
    slab_of,
    final_gain,
    row_order,
):
    groups = lax.axis_size("ex") * lax.axis_size("ez")
    row_count = attn_vals.shape[0]
    expert_count = router_weight.shape[1]
    slab_count = groups // expert_count
    partial_proj = jnp.dot(attn_vals, out_weight, preferred_element_type=jnp.float32)
    tensor_count = lax.axis_size("tensor")
    width = partial_proj.shape[1] // tensor_count
    pieces = partial_proj.astype(jnp.bfloat16).reshape(row_count, tensor_count, width)
    received = lax.all_to_all(
        pieces.transpose(1, 0, 2), "tensor", split_axis=0, concat_axis=0, tiled=True
    )
    project = jnp.sum(received.astype(jnp.float32), axis=0)
    stream_in = (residual.astype(jnp.float32) + project).astype(jnp.bfloat16)
    hidden_f = stream_in.astype(jnp.float32)
    scaled = hidden_f * norm_gain
    square_sum, logit_part = lax.psum(
        (
            jnp.sum(hidden_f * hidden_f, axis=1),
            jnp.dot(scaled, router_weight, precision=lax.Precision.HIGHEST),
        ),
        "tensor",
    )
    inverse_rms = lax.rsqrt(square_sum / D + EPS)
    logits = logit_part * inverse_rms[:, None]
    expert_ids = jnp.arange(expert_count, dtype=jnp.int32)
    route_hot = (routes[:, :, None] == expert_ids[None, None, :]).astype(jnp.int32)
    chosen = jnp.sum(route_hot.astype(jnp.float32) * logits[:, None, :], axis=2)
    leading = jax.nn.sigmoid(chosen[:, 0] - chosen[:, 1])
    mixing = jnp.stack([leading, 1.0 - leading], axis=1)
    route_hits = jnp.sum(route_hot, axis=1)
    before_count = jnp.cumsum(route_hits, axis=0) - route_hits
    slot_ids = jnp.sum(route_hot * before_count[:, None, :], axis=2)
    slot_hot = (slot_ids[:, :, None] == jnp.arange(MOST, dtype=jnp.int32)[None, None, :]).astype(
        jnp.float32
    )
    placing = jnp.einsum("rke,rks->esr", route_hot.astype(jnp.float32), slot_hot).astype(
        jnp.bfloat16
    )
    target_expert = slab_of // slab_count
    send_map = jnp.take(placing, target_expert, axis=0)
    outgoing = jnp.einsum(
        "gsr,rd->gsd", send_map, stream_in, preferred_element_type=jnp.float32
    ).astype(jnp.bfloat16)
    arrived_part = lax.all_to_all(outgoing, EXPERT, split_axis=0, concat_axis=0, tiled=True)
    arrived = lax.all_gather(arrived_part, "tensor", axis=2, tiled=True)
    part_f = arrived_part.astype(jnp.float32)
    slot_square = lax.psum(jnp.sum(part_f * part_f, axis=2), "tensor")
    slot_rms = lax.rsqrt(slot_square / D + EPS)[:, :, None]
    gain_full = lax.all_gather(norm_gain, "tensor", axis=0, tiled=True)[:, None]
    gate_weight = (w_gate[0].astype(jnp.float32) * gain_full).astype(jnp.bfloat16)
    up_weight = (w_up[0].astype(jnp.float32) * gain_full).astype(jnp.bfloat16)
    gate_val = slot_rms * jnp.einsum(
        "gmd,df->gmf", arrived, gate_weight, preferred_element_type=jnp.float32
    )
    up_val = slot_rms * jnp.einsum("gmd,df->gmf", arrived, up_weight, preferred_element_type=jnp.float32)
    returned = finish_slots(gate_val, up_val, w_down[0])
    group_ids = jnp.arange(groups, dtype=jnp.int32)
    holder_hot = (slab_of[None, :] == group_ids[:, None]).astype(jnp.int32)
    holders = jnp.sum(holder_hot * group_ids[None, :], axis=1).reshape(expert_count, slab_count)
    row_holders = jnp.take(holders, routes, axis=0)
    flat_index = row_holders * MOST + slot_ids[:, :, None]
    flat_back = returned.reshape(groups * MOST, returned.shape[2])
    fetched = jnp.take(flat_back, flat_index.reshape(-1), axis=0).reshape(
        row_count, 2, slab_count, returned.shape[2]
    )
    expert_out = jnp.sum(fetched.astype(jnp.float32), axis=2)
    blended = jnp.sum(mixing[:, :, None] * expert_out, axis=1)
    stream = (hidden_f + blended).astype(jnp.bfloat16)
    positions = (lax.axis_index("ex") * lax.axis_size("ez") + lax.axis_index("ez")) * row_count + jnp.arange(row_count, dtype=jnp.int32)
    matches = (row_order[None, :] == positions[:, None]).astype(jnp.int32)
    source = jnp.sum(matches * jnp.arange(row_order.shape[0], dtype=jnp.int32)[None, :], axis=1)
    ordered = restore(stream, row_order, source)
    return (ordered, final_norm(ordered, final_gain))


def outer_size(mesh):
    column = mesh.devices[:, 0]
    try:
        outer = len({d.coords[0] for d in column})
    except AttributeError:
        outer = 1
    if outer < 1 or column.shape[0] % outer:
        outer = 1
    return outer


def solution(mesh):
    outer = outer_size(mesh)
    shape = mesh.devices.shape
    split = Mesh(mesh.devices.reshape(outer, shape[0] // outer, shape[1]), ("ex", "ez", "tensor"))
    return jax.shard_map(
        on_device,
        mesh=split,
        in_specs=(
            P(EXPERT, "tensor"),
            P(EXPERT, "tensor"),
            P("tensor", None),
            P("tensor"),
            P("tensor", None),
            P(EXPERT, None),
            P(EXPERT, None, "tensor"),
            P(EXPERT, None, "tensor"),
            P(EXPERT, "tensor", None),
            P(),
            P("tensor"),
            P(),
        ),
        out_specs=(P(EXPERT, "tensor"), P(EXPERT, "tensor")),
        check_vma=False,
    )
```
